512 devices in a mesh: dp: 2 (over x_hi), blk: 32 (over z, x_lo, core), uly: 8 (over y).
Axes of the slice: x: 4 (x_hi: 2, x_lo: 2; x = x_hi * 2 + x_lo), y: 8, z: 8, core: 2. Of those that a mesh axis runs over, the one named last changes fastest.
Arguments:
- queries: bfloat16 [65536, 4096], P(('dp', 'blk', 'uly')), parts along dimension 0, may hold values from -24 to 24
- keys: bfloat16 [65536, 1024], P(('dp', 'blk', 'uly')), parts along dimension 0, may hold values from -12 to 12
- values: bfloat16 [65536, 1024], P(('dp', 'blk', 'uly')), parts along dimension 0, may hold values from -6 to 6
- doc_lengths: int32 [42], P('dp'), parts along dimension 0, may hold values from 1 to 2048, 32768 in all
Outputs:
- attended: bfloat16 [65536, 4096], P(('dp', 'blk', 'uly')), parts along dimension 0
The draws below stay inside these ranges and needn't reach their ends.
There are 2 independent parts, one for each index of `dp`. The reference program is written for one: setup_inputs(seed, part) draws one part's arguments, and reference() takes and returns one part's arrays. A program takes and returns all parts, laid end to end along the dimension named above; each array names one. Nothing has to cross between parts.
Inputs may be any that keep to these rules, and one draw needn't show every extreme that they name: `doc_lengths`: the 21 lengths sum to 32768; the longest is exactly 2048.
All inputs are finite; a program needn't handle non-finite values.
Results may differ from the reference program's by a relative error of at most 0.0055.
Values may be sent and summed in bfloat16 or wider, within the bound.
No kernel may reach another device: no remote copies, remote signals or barrier semaphores. Data moves between devices by JAX's collectives and lax.ppermute only.
A program may use at most 64 MiB of HBM per device.

```python
import math
import jax
import jax.numpy as jnp
import numpy as np
from jax import lax

QUERY_HEADS = 32
KEY_VALUE_HEADS = 8
HEAD_SIZE = 128
TOK_DEV = 128
CYCLE = 2
PACKED_TOKENS = 32768
DOC_MAX = 2048
DOCS = 21
N_BLK = 32
N_ULY = 8


def broadcast_keys(key):
    starting_offset = jax.random.normal(jax.random.fold_in(key, 7), (PACKED_TOKENS, KEY_VALUE_HEADS * HEAD_SIZE), jnp.float32)
    result = starting_offset
    return jnp.clip(result, -12.0, 12.0)


def draw_keys(key, part):
    return broadcast_keys(key).astype(jnp.bfloat16)


def draw_queries(key, part):
    own = jax.random.normal(jax.random.fold_in(key, 11), (PACKED_TOKENS, QUERY_HEADS * HEAD_SIZE), jnp.float32)
    return jnp.clip(own, -24.0, 24.0).astype(jnp.bfloat16)


def levels(own_key, dims, cuts, low, largest):
    def one(position, shards_of):
        draws = jax.random.uniform(jax.random.fold_in(jax.random.fold_in(own_key, 6), position), (shards_of,), jnp.float32, low / len(cuts), largest / len(cuts))
        return jnp.repeat(jnp.exp(draws), dims[position] // shards_of).reshape((-1,) + (1,) * (len(dims) - position - 1))

    level = one(*cuts[0])
    for cut in cuts[1:]:
        level = level * one(*cut)
    return level


def split_up(count, total, limit, lean):
    weights = [(1 << 20) // math.isqrt(standing ** lean) + 1 for standing in range(2, count + 1)]
    spare, holding = total - limit - (count - 1), [1] * (count - 1)
    while spare > 0:
        free = [i for i in range(count - 1) if holding[i] < limit]
        whole, left = sum([weights[i] for i in free]), spare
        for i in free:
            addition = min(limit - holding[i], max(1, left * weights[i] // whole), spare)
            holding[i] = holding[i] + addition
            spare = spare - addition
    return np.array([limit] + holding)


def ragged_sizes(key, amount, total, limit, lean):
    if amount == 2:
        one = jax.random.randint(key, (), max(1, total - limit), min(limit, total - 1) + 1)
        return jnp.stack([one, total - one])
    sizes = jnp.asarray(split_up(amount, total, limit, lean), jnp.int32)
    twos = (amount - 1) // 2
    giver, taker = sizes[1:1 + 2 * twos:2], sizes[2:2 + 2 * twos:2]
    room = jnp.minimum(giver - 1, limit - taker)
    passed = jax.random.randint(jax.random.fold_in(key, 1), (twos,), 0, 1 << 20) % (room + 1)
    sizes = sizes.at[1:1 + 2 * twos:2].set(giver - passed).at[2:2 + 2 * twos:2].set(taker + passed)
    return sizes[jax.random.permutation(jax.random.fold_in(key, 2), amount)]


def centred(own_key, dims, width, reach, cuts=(), kind=jnp.bfloat16):
    array = width * jax.random.normal(own_key, dims, jnp.float32)
    if cuts:
        array = array * levels(own_key, dims, cuts, -0.22, 0.18)
    return jnp.clip(array, -reach, reach).astype(kind)


def setup_inputs(seed: int = 0, part: int = 0) -> dict:
    seeds = jax.random.split(jax.random.key(seed), 5)
    part_splits = jax.random.split(jax.random.fold_in(seeds[4], part), 5)
    queries = draw_queries(jax.random.fold_in(jax.random.fold_in(seeds[4], part), 71), part)
    keys = draw_keys(jax.random.fold_in(jax.random.fold_in(seeds[4], part), 71), part)
    values = centred(part_splits[2], (PACKED_TOKENS, KEY_VALUE_HEADS * HEAD_SIZE), 1.0, 6.0, ((0, 256),))
    doc_lengths = ragged_sizes(part_splits[3], DOCS, PACKED_TOKENS, DOC_MAX, 2).astype(jnp.int32)
    return {"queries": queries, "keys": keys, "values": values, "doc_lengths": doc_lengths}


NEG_FILL = -1e+30

def reference(queries, keys, values, doc_lengths):
    block = TOK_DEV * N_ULY
    token_extent = CYCLE * block
    query_group = QUERY_HEADS // KEY_VALUE_HEADS
    total_rows = queries.shape[0]
    ends = jnp.cumsum(doc_lengths)

    def doc_of(positions):
        return lax.optimization_barrier(jnp.sum((positions[:, None] >= ends[None, :]).astype(jnp.int32), axis=1))
    q_all = queries.reshape(total_rows, QUERY_HEADS, HEAD_SIZE)
    padded_keys = jnp.concatenate([jnp.zeros((token_extent, KEY_VALUE_HEADS * HEAD_SIZE), keys.dtype), keys], axis=0).reshape(-1, KEY_VALUE_HEADS, HEAD_SIZE)
    padded_values = jnp.concatenate([jnp.zeros((token_extent, KEY_VALUE_HEADS * HEAD_SIZE), values.dtype), values], axis=0).reshape(-1, KEY_VALUE_HEADS, HEAD_SIZE)
    scale = 1.0 / math.sqrt(HEAD_SIZE)
    rows = jnp.arange(block, dtype=jnp.int32)
    cols = jnp.arange(token_extent + block, dtype=jnp.int32)

    def one_block(index):
        start = (index * block).astype(jnp.int32)
        q_block = lax.dynamic_slice_in_dim(q_all, start, block, 0).astype(jnp.float32)
        k_block = jnp.repeat(lax.dynamic_slice_in_dim(padded_keys, start, token_extent + block, 0).astype(jnp.float32), query_group, axis=1)
        v_block = jnp.repeat(lax.dynamic_slice_in_dim(padded_values, start, token_extent + block, 0).astype(jnp.float32), query_group, axis=1)
        q_pos = start + rows
        k_pos = start - token_extent + cols
        allowed = (k_pos[None, :] <= q_pos[:, None]) & (k_pos[None, :] >= 0) & (doc_of(k_pos)[None, :] == doc_of(q_pos)[:, None])
        scores = jnp.einsum('qhd,khd->hqk', q_block, k_block, precision=lax.Precision.HIGHEST) * scale
        scores = jnp.where(allowed[None], scores, NEG_FILL)
        peak = lax.optimization_barrier(jnp.max(scores, axis=-1, keepdims=True))
        weights = jnp.where(allowed[None], jnp.exp(scores - peak), 0.0)
        total = lax.optimization_barrier(jnp.sum(weights, axis=-1))
        rounded = lax.optimization_barrier(weights.astype(jnp.bfloat16)).astype(jnp.float32)
        summed = jnp.einsum('hqk,khd->qhd', rounded, v_block, precision=lax.Precision.HIGHEST)
        result = summed / jnp.transpose(total)[:, :, None]
        return result.astype(jnp.bfloat16).reshape(block, QUERY_HEADS * HEAD_SIZE)
    blocks = lax.map(one_block, jnp.arange(N_BLK, dtype=jnp.int32))
    return blocks.reshape(total_rows, QUERY_HEADS * HEAD_SIZE)
```

```python
import functools
import math

import jax
import jax.numpy as jnp
from jax import lax
from jax.experimental import pallas as pl
from jax.experimental.pallas import tpu as pltpu
from jax.sharding import PartitionSpec as P

QUERY_HEADS = 32
KEY_VALUE_HEADS = 8
HEAD_SIZE = 128
CYCLE = 2

Q_TILE = 256
K_TILE = 256

NEG_FILL = -1e30


def passed_along(block, axis, distance):
    devices = range(lax.axis_size(axis))
    route = [(i - distance, i) for i in devices if i - distance in devices]
    return lax.ppermute(block, axis, route)


def doc_index(positions, doc_lengths):
    ends = jnp.cumsum(doc_lengths)
    return jnp.sum((positions[:, None] >= ends[None, :]).astype(jnp.int32), axis=1)


def attend_kernel(bounds_ref, q_doc_ref, k_doc_ref, q_ref, k_ref, v_ref, o_ref,
                  peak_sc, total_sc, summed_sc, *, heads, ext_off):
    i = pl.program_id(0)
    lo = bounds_ref[2 * i]
    hi = bounds_ref[2 * i + 1]
    peak_sc[...] = jnp.full(peak_sc.shape, NEG_FILL, jnp.float32)
    total_sc[...] = jnp.zeros(total_sc.shape, jnp.float32)
    summed_sc[...] = jnp.zeros(summed_sc.shape, jnp.float32)
    q_doc = q_doc_ref[...]
    q_col = i * Q_TILE + ext_off + lax.broadcasted_iota(jnp.int32, (Q_TILE, 1), 0)
    scale = 1.0 / math.sqrt(HEAD_SIZE)

    def body(j, carry):
        start = pl.multiple_of(j * K_TILE, K_TILE)
        k = k_ref[pl.ds(start, K_TILE), :]
        v = v_ref[pl.ds(start, K_TILE), :]
        k_doc = k_doc_ref[pl.ds(j, 1), :]
        k_col = start + lax.broadcasted_iota(jnp.int32, (1, K_TILE), 1)
        allowed = (k_doc == q_doc) & (k_col <= q_col)
        for h in range(heads):
            q = q_ref[:, h * HEAD_SIZE:(h + 1) * HEAD_SIZE]
            scores = lax.dot_general(
                q, k, (((1,), (1,)), ((), ())), preferred_element_type=jnp.float32
            ) * scale
            scores = jnp.where(allowed, scores, NEG_FILL)
            peak = peak_sc[h]
            new_peak = jnp.maximum(peak, jnp.max(scores, axis=1, keepdims=True))
            weights = jnp.where(allowed, jnp.exp(scores - new_peak), 0.0)
            factor = jnp.exp(peak - new_peak)
            total_sc[h] = total_sc[h] * factor + jnp.sum(weights, axis=1, keepdims=True)
            summed_sc[h] = summed_sc[h] * factor + jnp.dot(
                weights.astype(jnp.bfloat16), v, preferred_element_type=jnp.float32
            )
            peak_sc[h] = new_peak
        return carry

    lax.fori_loop(lo, hi + 1, body, 0)
    for h in range(heads):
        o_ref[:, h * HEAD_SIZE:(h + 1) * HEAD_SIZE] = (
            summed_sc[h] / total_sc[h]
        ).astype(o_ref.dtype)


def attend(bounds, q_doc, k_doc, q2, k_ext, v_ext, heads, ext_off):
    rows = q2.shape[0]
    ext = k_ext.shape[0]
    n_q = rows // Q_TILE
    n_k = ext // K_TILE
    kernel = functools.partial(attend_kernel, heads=heads, ext_off=ext_off)
    grid_spec = pltpu.PrefetchScalarGridSpec(
        num_scalar_prefetch=1,
        grid=(n_q,),
        in_specs=[
            pl.BlockSpec((Q_TILE, 1), lambda i, b: (i, 0)),
            pl.BlockSpec((n_k, K_TILE), lambda i, b: (0, 0)),
            pl.BlockSpec((Q_TILE, heads * HEAD_SIZE), lambda i, b: (i, 0)),
            pl.BlockSpec((ext, HEAD_SIZE), lambda i, b: (0, 0)),
            pl.BlockSpec((ext, HEAD_SIZE), lambda i, b: (0, 0)),
        ],
        out_specs=pl.BlockSpec((Q_TILE, heads * HEAD_SIZE), lambda i, b: (i, 0)),
        scratch_shapes=[
            pltpu.VMEM((heads, Q_TILE, 1), jnp.float32),
            pltpu.VMEM((heads, Q_TILE, 1), jnp.float32),
            pltpu.VMEM((heads, Q_TILE, HEAD_SIZE), jnp.float32),
        ],
    )
    return pl.pallas_call(
        kernel,
        grid_spec=grid_spec,
        out_shape=jax.ShapeDtypeStruct((rows, heads * HEAD_SIZE), jnp.bfloat16),
    )(bounds, q_doc, k_doc, q2, k_ext, v_ext)


def tile_bounds(position, block, ext_off, ext, doc_lengths):
    ends = jnp.cumsum(doc_lengths)
    starts = ends - doc_lengths
    n_q = block // Q_TILE
    n_k = ext // K_TILE
    first = position * block + jnp.arange(n_q, dtype=jnp.int32) * Q_TILE
    first_doc = jnp.clip(doc_index(first, doc_lengths), 0, doc_lengths.shape[0] - 1)
    lo_key = starts[first_doc] - position * block + ext_off
    lo_key = jnp.maximum(lo_key, 0)
    hi_key = jnp.arange(n_q, dtype=jnp.int32) * Q_TILE + Q_TILE - 1 + ext_off
    hi = jnp.clip(hi_key // K_TILE, 0, n_k - 1)
    lo = jnp.clip(lo_key // K_TILE, 0, hi)
    return jnp.stack([lo, hi], axis=1).reshape(-1).astype(jnp.int32)


def per_device(queries, keys, values, doc_lengths):
    token_rows = queries.shape[0]
    q_heads = queries.reshape(token_rows, QUERY_HEADS, HEAD_SIZE)
    kv_heads = jnp.stack(
        [
            keys.reshape(token_rows, KEY_VALUE_HEADS, HEAD_SIZE),
            values.reshape(token_rows, KEY_VALUE_HEADS, HEAD_SIZE),
        ],
        axis=2,
    )
    q_local, kv_local = (
        lax.all_to_all(q_heads, "uly", split_axis=1, concat_axis=0, tiled=True),
        lax.all_to_all(kv_heads, "uly", split_axis=1, concat_axis=0, tiled=True),
    )
    block = q_local.shape[0]
    heads = q_local.shape[1]
    ext_off = CYCLE * block
    ext = ext_off + block
    position = lax.axis_index("blk")

    pieces = [kv_local]
    moving = kv_local
    for back in range(1, CYCLE + 1):
        moving = passed_along(moving, "blk", 1)
        pieces.append(moving)
    kv_ext = jnp.concatenate(pieces[::-1], axis=0)
    k_ext = kv_ext[:, 0, 0, :]
    v_ext = kv_ext[:, 0, 1, :]

    q_pos = position * block + jnp.arange(block, dtype=jnp.int32)
    q_doc = doc_index(q_pos, doc_lengths).reshape(block, 1)
    k_pos = position * block - ext_off + jnp.arange(ext, dtype=jnp.int32)
    k_doc = jnp.where(k_pos >= 0, doc_index(k_pos, doc_lengths), -1)
    k_doc = k_doc.reshape(ext // K_TILE, K_TILE)
    bounds = tile_bounds(position, block, ext_off, ext, doc_lengths)

    q2 = q_local.reshape(block, heads * HEAD_SIZE)
    result = attend(bounds, q_doc, k_doc, q2, k_ext, v_ext, heads, ext_off)
    result = result.reshape(block, heads, HEAD_SIZE)
    returned = lax.all_to_all(result, "uly", split_axis=0, concat_axis=1, tiled=True)
    return returned.reshape(token_rows, QUERY_HEADS * HEAD_SIZE)


def solution(mesh):
    in_specs = (
        P(("dp", "blk", "uly"), None),
        P(("dp", "blk", "uly"), None),
        P(("dp", "blk", "uly"), None),
        P("dp"),
    )
    out_specs = P(("dp", "blk", "uly"), None)
    return jax.shard_map(
        per_device, mesh=mesh, in_specs=in_specs, out_specs=out_specs, check_vma=False
    )
```

```python
import functools
import math

import jax
import jax.numpy as jnp
from jax import lax
from jax.experimental import pallas as pl
from jax.experimental.pallas import tpu as pltpu
from jax.sharding import PartitionSpec as P

QUERY_HEADS = 32
KEY_VALUE_HEADS = 8
HEAD_SIZE = 128
CYCLE = 2

Q_TILE = 128
K_TILE = 512

NEG_FILL = -1e30


def passed_along(block, axis, distance):
    devices = range(lax.axis_size(axis))
    route = [(i - distance, i) for i in devices if i - distance in devices]
    return lax.ppermute(block, axis, route)


def doc_index(positions, doc_lengths):
    ends = jnp.cumsum(doc_lengths)
    return jnp.sum((positions[:, None] >= ends[None, :]).astype(jnp.int32), axis=1)


def attend_kernel(bounds_ref, q_doc_ref, k_doc_ref, q_ref, k_ref, vt_ref, o_ref,
                  peak_sc, total_sc, summed_sc, *, heads, ext_off):
    i = pl.program_id(0)
    lo = bounds_ref[2 * i]
    hi = bounds_ref[2 * i + 1]
    peak_sc[...] = jnp.full(peak_sc.shape, NEG_FILL, jnp.float32)
    total_sc[...] = jnp.zeros(total_sc.shape, jnp.float32)
    summed_sc[...] = jnp.zeros(summed_sc.shape, jnp.float32)
    q_doc = q_doc_ref[...]
    q_col = i * Q_TILE + ext_off + lax.broadcasted_iota(jnp.int32, (1, Q_TILE), 1)
    rate = math.log2(math.e) / math.sqrt(HEAD_SIZE)

    def body(j, carry):
        start = pl.multiple_of(j * K_TILE, K_TILE)
        k = k_ref[pl.ds(start, K_TILE), :]
        vt = vt_ref[j]
        k_doc = k_doc_ref[pl.ds(start, K_TILE), :]
        k_row = start + lax.broadcasted_iota(jnp.int32, (K_TILE, 1), 0)
        bias = jnp.where((k_doc == q_doc) & (k_row <= q_col), 0.0, NEG_FILL)
        for h in range(heads):
            q = q_ref[:, h * HEAD_SIZE:(h + 1) * HEAD_SIZE]
            scores = lax.dot_general(
                k, q, (((1,), (1,)), ((), ())), preferred_element_type=jnp.float32
            ) + bias
            peak = peak_sc[h]
            new_peak = jnp.maximum(peak, jnp.max(scores, axis=0, keepdims=True))
            floor = jnp.maximum(new_peak, 0.1 * NEG_FILL)
            weights = jnp.exp2((scores - floor) * rate)
            factor = jnp.exp2((peak - new_peak) * rate)
            total_sc[h] = total_sc[h] * factor + jnp.sum(weights, axis=0, keepdims=True)
            summed_sc[h] = summed_sc[h] * factor + jnp.dot(
                vt, weights.astype(jnp.bfloat16), preferred_element_type=jnp.float32
            )
            peak_sc[h] = new_peak
        return carry

    lax.fori_loop(lo, hi + 1, body, 0)
    for h in range(heads):
        o_ref[:, h * HEAD_SIZE:(h + 1) * HEAD_SIZE] = (
            (summed_sc[h] / total_sc[h]).T
        ).astype(o_ref.dtype)


def attend(bounds, q_doc, k_doc, q2, k_ext, vt_ext, heads, ext_off):
    rows = q2.shape[0]
    ext = k_ext.shape[0]
    n_q = rows // Q_TILE
    n_k = ext // K_TILE
    kernel = functools.partial(attend_kernel, heads=heads, ext_off=ext_off)
    grid_spec = pltpu.PrefetchScalarGridSpec(
        num_scalar_prefetch=1,
        grid=(n_q,),
        in_specs=[
            pl.BlockSpec((1, Q_TILE), lambda i, b: (0, i)),
            pl.BlockSpec((ext, 1), lambda i, b: (0, 0)),
            pl.BlockSpec((Q_TILE, heads * HEAD_SIZE), lambda i, b: (i, 0)),
            pl.BlockSpec((ext, HEAD_SIZE), lambda i, b: (0, 0)),
            pl.BlockSpec((n_k, HEAD_SIZE, K_TILE), lambda i, b: (0, 0, 0)),
        ],
        out_specs=pl.BlockSpec((Q_TILE, heads * HEAD_SIZE), lambda i, b: (i, 0)),
        scratch_shapes=[
            pltpu.VMEM((heads, 1, Q_TILE), jnp.float32),
            pltpu.VMEM((heads, 1, Q_TILE), jnp.float32),
            pltpu.VMEM((heads, HEAD_SIZE, Q_TILE), jnp.float32),
        ],
    )
    return pl.pallas_call(
        kernel,
        grid_spec=grid_spec,
        out_shape=jax.ShapeDtypeStruct((rows, heads * HEAD_SIZE), jnp.bfloat16),
        compiler_params=pltpu.CompilerParams(),
    )(bounds, q_doc, k_doc, q2, k_ext, vt_ext)


def tile_bounds(position, block, ext_off, ext, doc_lengths):
    ends = jnp.cumsum(doc_lengths)
    starts = ends - doc_lengths
    n_q = block // Q_TILE
    n_k = ext // K_TILE
    first = position * block + jnp.arange(n_q, dtype=jnp.int32) * Q_TILE
    first_doc = jnp.clip(doc_index(first, doc_lengths), 0, doc_lengths.shape[0] - 1)
    lo_key = starts[first_doc] - position * block + ext_off
    lo_key = jnp.maximum(lo_key, 0)
    hi_key = jnp.arange(n_q, dtype=jnp.int32) * Q_TILE + Q_TILE - 1 + ext_off
    hi = jnp.clip(hi_key // K_TILE, 0, n_k - 1)
    lo = jnp.clip(lo_key // K_TILE, 0, hi)
    return jnp.stack([lo, hi], axis=1).reshape(-1).astype(jnp.int32)


def per_device(queries, keys, values, doc_lengths):
    token_rows = queries.shape[0]
    q_heads = queries.reshape(token_rows, QUERY_HEADS, HEAD_SIZE)
    kv_heads = jnp.stack(
        [
            keys.reshape(token_rows, KEY_VALUE_HEADS, HEAD_SIZE),
            values.reshape(token_rows, KEY_VALUE_HEADS, HEAD_SIZE),
        ],
        axis=2,
    )
    q_local, kv_local = (
        lax.all_to_all(q_heads, "uly", split_axis=1, concat_axis=0, tiled=True),
        lax.all_to_all(kv_heads, "uly", split_axis=1, concat_axis=0, tiled=True),
    )
    block = q_local.shape[0]
    heads = q_local.shape[1]
    ext_off = CYCLE * block
    ext = ext_off + block
    position = lax.axis_index("blk")

    pieces = [kv_local]
    moving = kv_local
    for back in range(1, CYCLE + 1):
        moving = passed_along(moving, "blk", 1)
        pieces.append(moving)
    kv_ext = jnp.concatenate(pieces[::-1], axis=0)
    k_ext = kv_ext[:, 0, 0, :]
    v_ext = kv_ext[:, 0, 1, :]

    q_pos = position * block + jnp.arange(block, dtype=jnp.int32)
    q_doc = doc_index(q_pos, doc_lengths).reshape(1, block)
    k_pos = position * block - ext_off + jnp.arange(ext, dtype=jnp.int32)
    k_doc = jnp.where(k_pos >= 0, doc_index(k_pos, doc_lengths), -1)
    k_doc = k_doc.reshape(ext, 1)
    bounds = tile_bounds(position, block, ext_off, ext, doc_lengths)

    q2 = q_local.reshape(block, heads * HEAD_SIZE)
    vt_ext = v_ext.reshape(ext // K_TILE, K_TILE, HEAD_SIZE).transpose(0, 2, 1)
    result = attend(bounds, q_doc, k_doc, q2, k_ext, vt_ext, heads, ext_off)
    result = result.reshape(block, heads, HEAD_SIZE)
    returned = lax.all_to_all(result, "uly", split_axis=0, concat_axis=1, tiled=True)
    return returned.reshape(token_rows, QUERY_HEADS * HEAD_SIZE)


def solution(mesh):
    in_specs = (
        P(("dp", "blk", "uly"), None),
        P(("dp", "blk", "uly"), None),
        P(("dp", "blk", "uly"), None),
        P("dp"),
    )
    out_specs = P(("dp", "blk", "uly"), None)
    return jax.shard_map(
        per_device, mesh=mesh, in_specs=in_specs, out_specs=out_specs, check_vma=False
    )
```

```python
import functools
import math

import jax
import jax.numpy as jnp
from jax import lax
from jax.experimental import pallas as pl
from jax.experimental.pallas import tpu as pltpu
from jax.sharding import PartitionSpec as P

QUERY_HEADS = 32
KEY_VALUE_HEADS = 8
HEAD_SIZE = 128
CYCLE = 2

Q_TILE = 128
K_TILE = 512
SPLITS = 2

NEG_FILL = -1e30


def passed_along(block, axis, distance):
    devices = range(lax.axis_size(axis))
    route = [(i - distance, i) for i in devices if i - distance in devices]
    return lax.ppermute(block, axis, route)


def doc_index(positions, doc_lengths):
    ends = jnp.cumsum(doc_lengths)
    return jnp.sum((positions[:, None] >= ends[None, :]).astype(jnp.int32), axis=1)


def attend_kernel(bounds_ref, q_doc_ref, k_doc_ref, q_ref, k_ref, vt_ref, o_ref,
                  peak_sc, total_sc, summed_sc, *, heads, ext_off):
    i = pl.program_id(0)
    lo = bounds_ref[2 * i]
    hi = bounds_ref[2 * i + 1]
    peak_sc[...] = jnp.full(peak_sc.shape, NEG_FILL, jnp.float32)
    total_sc[...] = jnp.zeros(total_sc.shape, jnp.float32)
    summed_sc[...] = jnp.zeros(summed_sc.shape, jnp.float32)
    q_doc = q_doc_ref[...]
    q_col = i * Q_TILE + ext_off + lax.broadcasted_iota(jnp.int32, (1, Q_TILE), 1)
    rate = math.log2(math.e) / math.sqrt(HEAD_SIZE)

    def body(j, carry):
        start = pl.multiple_of(j * K_TILE, K_TILE)
        k = k_ref[pl.ds(start, K_TILE), :]
        vt = vt_ref[j]
        k_doc = k_doc_ref[pl.ds(start, K_TILE), :]
        k_row = start + lax.broadcasted_iota(jnp.int32, (K_TILE, 1), 0)
        bias = jnp.where((k_doc == q_doc) & (k_row <= q_col), 0.0, NEG_FILL)
        for h in range(heads):
            q = q_ref[:, h * HEAD_SIZE:(h + 1) * HEAD_SIZE]
            scores = lax.dot_general(
                k, q, (((1,), (1,)), ((), ())), preferred_element_type=jnp.float32
            ) + bias
            peak = peak_sc[h]
            new_peak = jnp.maximum(peak, jnp.max(scores, axis=0, keepdims=True))
            floor = jnp.maximum(new_peak, 0.1 * NEG_FILL)
            weights = jnp.exp2((scores - floor) * rate)
            factor = jnp.exp2((peak - new_peak) * rate)
            total_sc[h] = total_sc[h] * factor + jnp.sum(weights, axis=0, keepdims=True)
            summed_sc[h] = summed_sc[h] * factor + jnp.dot(
                vt, weights.astype(jnp.bfloat16), preferred_element_type=jnp.float32
            )
            peak_sc[h] = new_peak
        return carry

    lax.fori_loop(lo, hi + 1, body, 0)
    for h in range(heads):
        o_ref[:, h * HEAD_SIZE:(h + 1) * HEAD_SIZE] = (
            (summed_sc[h] / total_sc[h]).T
        ).astype(o_ref.dtype)


def attend(bounds, q_doc, k_doc, q2, k_ext, vt_ext, heads, ext_off):
    rows = q2.shape[0]
    ext = k_ext.shape[0]
    n_q = rows // Q_TILE
    n_k = ext // K_TILE
    kernel = functools.partial(attend_kernel, heads=heads, ext_off=ext_off)
    grid_spec = pltpu.PrefetchScalarGridSpec(
        num_scalar_prefetch=1,
        grid=(n_q,),
        in_specs=[
            pl.BlockSpec((1, Q_TILE), lambda i, b: (0, i)),
            pl.BlockSpec((ext, 1), lambda i, b: (0, 0)),
            pl.BlockSpec((Q_TILE, heads * HEAD_SIZE), lambda i, b: (i, 0)),
            pl.BlockSpec((ext, HEAD_SIZE), lambda i, b: (0, 0)),
            pl.BlockSpec((n_k, HEAD_SIZE, K_TILE), lambda i, b: (0, 0, 0)),
        ],
        out_specs=pl.BlockSpec((Q_TILE, heads * HEAD_SIZE), lambda i, b: (i, 0)),
        scratch_shapes=[
            pltpu.VMEM((heads, 1, Q_TILE), jnp.float32),
            pltpu.VMEM((heads, 1, Q_TILE), jnp.float32),
            pltpu.VMEM((heads, HEAD_SIZE, Q_TILE), jnp.float32),
        ],
    )
    return pl.pallas_call(
        kernel,
        grid_spec=grid_spec,
        out_shape=jax.ShapeDtypeStruct((rows, heads * HEAD_SIZE), jnp.bfloat16),
        compiler_params=pltpu.CompilerParams(),
    )(bounds, q_doc, k_doc, q2, k_ext, vt_ext)


def tile_bounds(position, block, ext_off, ext, doc_lengths):
    ends = jnp.cumsum(doc_lengths)
    starts = ends - doc_lengths
    n_q = block // Q_TILE
    n_k = ext // K_TILE
    first = position * block + jnp.arange(n_q, dtype=jnp.int32) * Q_TILE
    first_doc = jnp.clip(doc_index(first, doc_lengths), 0, doc_lengths.shape[0] - 1)
    lo_key = starts[first_doc] - position * block + ext_off
    lo_key = jnp.maximum(lo_key, 0)
    hi_key = jnp.arange(n_q, dtype=jnp.int32) * Q_TILE + Q_TILE - 1 + ext_off
    hi = jnp.clip(hi_key // K_TILE, 0, n_k - 1)
    lo = jnp.clip(lo_key // K_TILE, 0, hi)
    return jnp.stack([lo, hi], axis=1).reshape(-1).astype(jnp.int32)


def per_device(queries, keys, values, doc_lengths):
    token_rows = queries.shape[0]
    kv_heads = jnp.stack(
        [
            keys.reshape(token_rows, KEY_VALUE_HEADS, HEAD_SIZE),
            values.reshape(token_rows, KEY_VALUE_HEADS, HEAD_SIZE),
        ],
        axis=2,
    )
    kv_local = lax.all_to_all(kv_heads, "uly", split_axis=1, concat_axis=0, tiled=True)
    block = kv_local.shape[0]
    ext_off = CYCLE * block
    ext = ext_off + block
    position = lax.axis_index("blk")

    pieces = [kv_local]
    moving = kv_local
    for back in range(1, CYCLE + 1):
        moving = passed_along(moving, "blk", 1)
        pieces.append(moving)
    kv_ext = jnp.concatenate(pieces[::-1], axis=0)
    k_ext = kv_ext[:, 0, 0, :]
    v_ext = kv_ext[:, 0, 1, :]

    q_pos = position * block + jnp.arange(block, dtype=jnp.int32)
    q_doc = doc_index(q_pos, doc_lengths).reshape(1, block)
    k_pos = position * block - ext_off + jnp.arange(ext, dtype=jnp.int32)
    k_doc = jnp.where(k_pos >= 0, doc_index(k_pos, doc_lengths), -1)
    k_doc = k_doc.reshape(ext, 1)
    bounds = tile_bounds(position, block, ext_off, ext, doc_lengths)
    vt_ext = v_ext.reshape(ext // K_TILE, K_TILE, HEAD_SIZE).transpose(0, 2, 1)

    group_repeat = QUERY_HEADS // KEY_VALUE_HEADS
    q_groups = queries.reshape(token_rows, KEY_VALUE_HEADS, group_repeat, HEAD_SIZE)
    step = group_repeat // SPLITS
    outs = []
    for part in range(SPLITS):
        q_part = q_groups[:, :, part * step:(part + 1) * step, :]
        q_local = lax.all_to_all(q_part, "uly", split_axis=1, concat_axis=0, tiled=True)
        q2 = q_local.reshape(block, step * HEAD_SIZE)
        result = attend(bounds, q_doc, k_doc, q2, k_ext, vt_ext, step, ext_off)
        result = result.reshape(block, 1, step, HEAD_SIZE)
        outs.append(lax.all_to_all(result, "uly", split_axis=0, concat_axis=1, tiled=True))
    returned = jnp.concatenate(outs, axis=2)
    return returned.reshape(token_rows, QUERY_HEADS * HEAD_SIZE)


def solution(mesh):
    in_specs = (
        P(("dp", "blk", "uly"), None),
        P(("dp", "blk", "uly"), None),
        P(("dp", "blk", "uly"), None),
        P("dp"),
    )
    out_specs = P(("dp", "blk", "uly"), None)
    return jax.shard_map(
        per_device, mesh=mesh, in_specs=in_specs, out_specs=out_specs, check_vma=False
    )
```

```python
import functools
import math

import jax
import jax.numpy as jnp
from jax import lax
from jax.experimental import pallas as pl
from jax.experimental.pallas import tpu as pltpu
from jax.sharding import PartitionSpec as P

QUERY_HEADS = 32
KEY_VALUE_HEADS = 8
HEAD_SIZE = 128
CYCLE = 2

Q_TILE = 256
K_TILE = 512
SPLITS = 2

NEG_FILL = -1e30


def passed_along(block, axis, distance):
    devices = range(lax.axis_size(axis))
    route = [(i - distance, i) for i in devices if i - distance in devices]
    return lax.ppermute(block, axis, route)


def doc_index(positions, doc_lengths):
    ends = jnp.cumsum(doc_lengths)
    return jnp.sum((positions[:, None] >= ends[None, :]).astype(jnp.int32), axis=1)


def attend_kernel(bounds_ref, q_doc_ref, k_doc_ref, q_ref, k_ref, vt_ref, o_ref,
                  peak_sc, total_sc, summed_sc, *, heads, ext_off):
    i = pl.program_id(0)
    lo = bounds_ref[2 * i]
    hi = bounds_ref[2 * i + 1]
    peak_sc[...] = jnp.full(peak_sc.shape, NEG_FILL, jnp.float32)
    total_sc[...] = jnp.zeros(total_sc.shape, jnp.float32)
    summed_sc[...] = jnp.zeros(summed_sc.shape, jnp.float32)
    q_doc = q_doc_ref[...]
    q_col = i * Q_TILE + ext_off + lax.broadcasted_iota(jnp.int32, (1, Q_TILE), 1)
    rate = math.log2(math.e) / math.sqrt(HEAD_SIZE)

    def body(j, carry):
        start = pl.multiple_of(j * K_TILE, K_TILE)
        k = k_ref[pl.ds(start, K_TILE), :]
        vt = vt_ref[j]
        k_doc = k_doc_ref[pl.ds(start, K_TILE), :]
        k_row = start + lax.broadcasted_iota(jnp.int32, (K_TILE, 1), 0)
        bias = jnp.where((k_doc == q_doc) & (k_row <= q_col), 0.0, NEG_FILL)
        for h in range(heads):
            q = q_ref[:, h * HEAD_SIZE:(h + 1) * HEAD_SIZE]
            scores = lax.dot_general(
                k, q, (((1,), (1,)), ((), ())), preferred_element_type=jnp.float32
            ) + bias
            peak = peak_sc[h]
            new_peak = jnp.maximum(peak, jnp.max(scores, axis=0, keepdims=True))
            floor = jnp.maximum(new_peak, 0.1 * NEG_FILL)
            weights = jnp.exp2((scores - floor) * rate)
            factor = jnp.exp2((peak - new_peak) * rate)
            total_sc[h] = total_sc[h] * factor + jnp.sum(weights, axis=0, keepdims=True)
            summed_sc[h] = summed_sc[h] * factor + jnp.dot(
                vt, weights.astype(jnp.bfloat16), preferred_element_type=jnp.float32
            )
            peak_sc[h] = new_peak
        return carry

    lax.fori_loop(lo, hi + 1, body, 0)
    for h in range(heads):
        o_ref[:, h * HEAD_SIZE:(h + 1) * HEAD_SIZE] = (
            (summed_sc[h] / total_sc[h]).T
        ).astype(o_ref.dtype)


def attend(bounds, q_doc, k_doc, q2, k_ext, vt_ext, heads, ext_off):
    rows = q2.shape[0]
    ext = k_ext.shape[0]
    n_q = rows // Q_TILE
    n_k = ext // K_TILE
    kernel = functools.partial(attend_kernel, heads=heads, ext_off=ext_off)
    grid_spec = pltpu.PrefetchScalarGridSpec(
        num_scalar_prefetch=1,
        grid=(n_q,),
        in_specs=[
            pl.BlockSpec((1, Q_TILE), lambda i, b: (0, i)),
            pl.BlockSpec((ext, 1), lambda i, b: (0, 0)),
            pl.BlockSpec((Q_TILE, heads * HEAD_SIZE), lambda i, b: (i, 0)),
            pl.BlockSpec((ext, HEAD_SIZE), lambda i, b: (0, 0)),
            pl.BlockSpec((n_k, HEAD_SIZE, K_TILE), lambda i, b: (0, 0, 0)),
        ],
        out_specs=pl.BlockSpec((Q_TILE, heads * HEAD_SIZE), lambda i, b: (i, 0)),
        scratch_shapes=[
            pltpu.VMEM((heads, 1, Q_TILE), jnp.float32),
            pltpu.VMEM((heads, 1, Q_TILE), jnp.float32),
            pltpu.VMEM((heads, HEAD_SIZE, Q_TILE), jnp.float32),
        ],
    )
    return pl.pallas_call(
        kernel,
        grid_spec=grid_spec,
        out_shape=jax.ShapeDtypeStruct((rows, heads * HEAD_SIZE), jnp.bfloat16),
        compiler_params=pltpu.CompilerParams(),
    )(bounds, q_doc, k_doc, q2, k_ext, vt_ext)


def tile_bounds(position, block, ext_off, ext, doc_lengths):
    ends = jnp.cumsum(doc_lengths)
    starts = ends - doc_lengths
    n_q = block // Q_TILE
    n_k = ext // K_TILE
    first = position * block + jnp.arange(n_q, dtype=jnp.int32) * Q_TILE
    first_doc = jnp.clip(doc_index(first, doc_lengths), 0, doc_lengths.shape[0] - 1)
    lo_key = starts[first_doc] - position * block + ext_off
    lo_key = jnp.maximum(lo_key, 0)
    hi_key = jnp.arange(n_q, dtype=jnp.int32) * Q_TILE + Q_TILE - 1 + ext_off
    hi = jnp.clip(hi_key // K_TILE, 0, n_k - 1)
    lo = jnp.clip(lo_key // K_TILE, 0, hi)
    return jnp.stack([lo, hi], axis=1).reshape(-1).astype(jnp.int32)


def per_device(queries, keys, values, doc_lengths):
    token_rows = queries.shape[0]
    kv_heads = jnp.stack(
        [
            keys.reshape(token_rows, KEY_VALUE_HEADS, HEAD_SIZE),
            values.reshape(token_rows, KEY_VALUE_HEADS, HEAD_SIZE),
        ],
        axis=2,
    )
    kv_local = lax.all_to_all(kv_heads, "uly", split_axis=1, concat_axis=0, tiled=True)
    block = kv_local.shape[0]
    ext_off = CYCLE * block
    ext = ext_off + block
    position = lax.axis_index("blk")

    pieces = [kv_local]
    for back in range(1, CYCLE + 1):
        pieces.append(passed_along(kv_local, "blk", back))
    kv_ext = jnp.concatenate(pieces[::-1], axis=0)
    k_ext = kv_ext[:, 0, 0, :]
    v_ext = kv_ext[:, 0, 1, :]

    q_pos = position * block + jnp.arange(block, dtype=jnp.int32)
    q_doc = doc_index(q_pos, doc_lengths).reshape(1, block)
    k_pos = position * block - ext_off + jnp.arange(ext, dtype=jnp.int32)
    k_doc = jnp.where(k_pos >= 0, doc_index(k_pos, doc_lengths), -1)
    k_doc = k_doc.reshape(ext, 1)
    bounds = tile_bounds(position, block, ext_off, ext, doc_lengths)
    vt_ext = v_ext.reshape(ext // K_TILE, K_TILE, HEAD_SIZE).transpose(0, 2, 1)

    group_repeat = QUERY_HEADS // KEY_VALUE_HEADS
    q_groups = queries.reshape(token_rows, KEY_VALUE_HEADS, group_repeat, HEAD_SIZE)
    step = group_repeat // SPLITS
    outs = []
    for part in range(SPLITS):
        q_part = q_groups[:, :, part * step:(part + 1) * step, :]
        q_local = lax.all_to_all(q_part, "uly", split_axis=1, concat_axis=0, tiled=True)
        q2 = q_local.reshape(block, step * HEAD_SIZE)
        result = attend(bounds, q_doc, k_doc, q2, k_ext, vt_ext, step, ext_off)
        result = result.reshape(block, 1, step, HEAD_SIZE)
        outs.append(lax.all_to_all(result, "uly", split_axis=0, concat_axis=1, tiled=True))
    returned = jnp.concatenate(outs, axis=2)
    return returned.reshape(token_rows, QUERY_HEADS * HEAD_SIZE)


def solution(mesh):
    in_specs = (
        P(("dp", "blk", "uly"), None),
        P(("dp", "blk", "uly"), None),
        P(("dp", "blk", "uly"), None),
        P("dp"),
    )
    out_specs = P(("dp", "blk", "uly"), None)
    return jax.shard_map(
        per_device, mesh=mesh, in_specs=in_specs, out_specs=out_specs, check_vma=False
    )
```

```python
import functools
import math

import jax
import jax.numpy as jnp
from jax import lax
from jax.experimental import pallas as pl
from jax.experimental.pallas import tpu as pltpu
from jax.sharding import PartitionSpec as P

QUERY_HEADS = 32
KEY_VALUE_HEADS = 8
HEAD_SIZE = 128
CYCLE = 2

Q_TILE = 128
K_TILE = 512

NEG_FILL = -1e30


def passed_along(block, axis, distance):
    devices = range(lax.axis_size(axis))
    route = [(i - distance, i) for i in devices if i - distance in devices]
    return lax.ppermute(block, axis, route)


def doc_index(positions, doc_lengths):
    ends = jnp.cumsum(doc_lengths)
    return jnp.sum((positions[:, None] >= ends[None, :]).astype(jnp.int32), axis=1)


def attend_kernel(bounds_ref, q_doc_ref, k_doc_ref, q_ref, k_ref, vt_ref, o_ref,
                  peak_sc, total_sc, summed_sc, *, heads, ext_off):
    i = pl.program_id(0)
    lo = bounds_ref[2 * i]
    hi = bounds_ref[2 * i + 1]
    peak_sc[...] = jnp.full(peak_sc.shape, NEG_FILL, jnp.float32)
    total_sc[...] = jnp.zeros(total_sc.shape, jnp.float32)
    summed_sc[...] = jnp.zeros(summed_sc.shape, jnp.float32)
    q_doc = q_doc_ref[...]
    q_col = i * Q_TILE + ext_off + lax.broadcasted_iota(jnp.int32, (1, Q_TILE), 1)
    rate = math.log2(math.e) / math.sqrt(HEAD_SIZE)

    def body(j, carry):
        start = pl.multiple_of(j * K_TILE, K_TILE)
        k = k_ref[pl.ds(start, K_TILE), :]
        vt = vt_ref[j]
        k_doc = k_doc_ref[pl.ds(start, K_TILE), :]
        k_row = start + lax.broadcasted_iota(jnp.int32, (K_TILE, 1), 0)
        bias = jnp.where((k_doc == q_doc) & (k_row <= q_col), 0.0, NEG_FILL)
        for h in range(heads):
            q = q_ref[:, h * HEAD_SIZE:(h + 1) * HEAD_SIZE]
            scores = lax.dot_general(
                k, q, (((1,), (1,)), ((), ())), preferred_element_type=jnp.float32
            ) + bias
            peak = peak_sc[h]
            new_peak = jnp.maximum(peak, jnp.max(scores, axis=0, keepdims=True))
            floor = jnp.maximum(new_peak, 0.1 * NEG_FILL)
            weights = jnp.exp2((scores - floor) * rate)
            factor = jnp.exp2((peak - new_peak) * rate)
            total_sc[h] = total_sc[h] * factor + jnp.sum(weights, axis=0, keepdims=True)
            summed_sc[h] = summed_sc[h] * factor + jnp.dot(
                vt, weights.astype(jnp.bfloat16), preferred_element_type=jnp.float32
            )
            peak_sc[h] = new_peak
        return carry

    lax.fori_loop(lo, hi + 1, body, 0)
    for h in range(heads):
        o_ref[:, h * HEAD_SIZE:(h + 1) * HEAD_SIZE] = (
            (summed_sc[h] / total_sc[h]).T
        ).astype(o_ref.dtype)


def attend(bounds, q_doc, k_doc, q2, k_ext, vt_ext, heads, ext_off):
    rows = q2.shape[0]
    ext = k_ext.shape[0]
    n_q = rows // Q_TILE
    n_k = ext // K_TILE
    kernel = functools.partial(attend_kernel, heads=heads, ext_off=ext_off)
    grid_spec = pltpu.PrefetchScalarGridSpec(
        num_scalar_prefetch=1,
        grid=(n_q,),
        in_specs=[
            pl.BlockSpec((1, Q_TILE), lambda i, b: (0, i)),
            pl.BlockSpec((ext, 1), lambda i, b: (0, 0)),
            pl.BlockSpec((Q_TILE, heads * HEAD_SIZE), lambda i, b: (i, 0)),
            pl.BlockSpec((ext, HEAD_SIZE), lambda i, b: (0, 0)),
            pl.BlockSpec((n_k, HEAD_SIZE, K_TILE), lambda i, b: (0, 0, 0)),
        ],
        out_specs=pl.BlockSpec((Q_TILE, heads * HEAD_SIZE), lambda i, b: (i, 0)),
        scratch_shapes=[
            pltpu.VMEM((heads, 1, Q_TILE), jnp.float32),
            pltpu.VMEM((heads, 1, Q_TILE), jnp.float32),
            pltpu.VMEM((heads, HEAD_SIZE, Q_TILE), jnp.float32),
        ],
    )
    return pl.pallas_call(
        kernel,
        grid_spec=grid_spec,
        out_shape=jax.ShapeDtypeStruct((rows, heads * HEAD_SIZE), jnp.bfloat16),
        compiler_params=pltpu.CompilerParams(),
    )(bounds, q_doc, k_doc, q2, k_ext, vt_ext)


def tile_bounds(position, block, ext_off, ext, doc_lengths):
    ends = jnp.cumsum(doc_lengths)
    starts = ends - doc_lengths
    n_q = block // Q_TILE
    n_k = ext // K_TILE
    first = position * block + jnp.arange(n_q, dtype=jnp.int32) * Q_TILE
    first_doc = jnp.clip(doc_index(first, doc_lengths), 0, doc_lengths.shape[0] - 1)
    lo_key = starts[first_doc] - position * block + ext_off
    lo_key = jnp.maximum(lo_key, 0)
    hi_key = jnp.arange(n_q, dtype=jnp.int32) * Q_TILE + Q_TILE - 1 + ext_off
    hi = jnp.clip(hi_key // K_TILE, 0, n_k - 1)
    lo = jnp.clip(lo_key // K_TILE, 0, hi)
    return jnp.stack([lo, hi], axis=1).reshape(-1).astype(jnp.int32)


def per_device(queries, keys, values, doc_lengths):
    token_rows = queries.shape[0]
    q_heads = queries.reshape(token_rows, QUERY_HEADS, HEAD_SIZE)
    kv_heads = jnp.stack(
        [
            keys.reshape(token_rows, KEY_VALUE_HEADS, HEAD_SIZE),
            values.reshape(token_rows, KEY_VALUE_HEADS, HEAD_SIZE),
        ],
        axis=2,
    )
    q_local, kv_local = (
        lax.all_to_all(q_heads, "uly", split_axis=1, concat_axis=0, tiled=True),
        lax.all_to_all(kv_heads, "uly", split_axis=1, concat_axis=0, tiled=True),
    )
    block = q_local.shape[0]
    heads = q_local.shape[1]
    ext_off = CYCLE * block
    ext = ext_off + block
    position = lax.axis_index("blk")

    pieces = [kv_local]
    for back in range(1, CYCLE + 1):
        pieces.append(passed_along(kv_local, "blk", back))
    kv_ext = jnp.concatenate(pieces[::-1], axis=0)
    k_ext = kv_ext[:, 0, 0, :]
    v_ext = kv_ext[:, 0, 1, :]

    q_pos = position * block + jnp.arange(block, dtype=jnp.int32)
    q_doc = doc_index(q_pos, doc_lengths).reshape(1, block)
    k_pos = position * block - ext_off + jnp.arange(ext, dtype=jnp.int32)
    k_doc = jnp.where(k_pos >= 0, doc_index(k_pos, doc_lengths), -1)
    k_doc = k_doc.reshape(ext, 1)
    bounds = tile_bounds(position, block, ext_off, ext, doc_lengths)

    q2 = q_local.reshape(block, heads * HEAD_SIZE)
    vt_ext = v_ext.reshape(ext // K_TILE, K_TILE, HEAD_SIZE).transpose(0, 2, 1)
    result = attend(bounds, q_doc, k_doc, q2, k_ext, vt_ext, heads, ext_off)
    result = result.reshape(block, heads, HEAD_SIZE)
    returned = lax.all_to_all(result, "uly", split_axis=0, concat_axis=1, tiled=True)
    return returned.reshape(token_rows, QUERY_HEADS * HEAD_SIZE)


def solution(mesh):
    in_specs = (
        P(("dp", "blk", "uly"), None),
        P(("dp", "blk", "uly"), None),
        P(("dp", "blk", "uly"), None),
        P("dp"),
    )
    out_specs = P(("dp", "blk", "uly"), None)
    return jax.shard_map(
        per_device, mesh=mesh, in_specs=in_specs, out_specs=out_specs, check_vma=False
    )
```

```python
import functools
import math

import jax
import jax.numpy as jnp
from jax import lax
from jax.experimental import pallas as pl
from jax.experimental.pallas import tpu as pltpu
from jax.sharding import PartitionSpec as P

QUERY_HEADS = 32
KEY_VALUE_HEADS = 8
HEAD_SIZE = 128
CYCLE = 2

Q_TILE = 128
K_TILE = 512
SPLITS = 2

NEG_FILL = -1e30


def passed_along(block, axis, distance):
    devices = range(lax.axis_size(axis))
    route = [(i - distance, i) for i in devices if i - distance in devices]
    return lax.ppermute(block, axis, route)


def doc_index(positions, doc_lengths):
    ends = jnp.cumsum(doc_lengths)
    return jnp.sum((positions[:, None] >= ends[None, :]).astype(jnp.int32), axis=1)


def attend_kernel(bounds_ref, q_doc_ref, q_col_ref, k_doc_ref, q_ref, k_ref, vt_ref, o_ref,
                  peak_sc, total_sc, summed_sc, *, heads, ext_off):
    i = pl.program_id(0)
    lo = bounds_ref[2 * i]
    hi = bounds_ref[2 * i + 1]
    peak_sc[...] = jnp.full(peak_sc.shape, NEG_FILL, jnp.float32)
    total_sc[...] = jnp.zeros(total_sc.shape, jnp.float32)
    summed_sc[...] = jnp.zeros(summed_sc.shape, jnp.float32)
    q_doc = q_doc_ref[...]
    q_col = q_col_ref[...]
    rate = math.log2(math.e) / math.sqrt(HEAD_SIZE)

    def body(j, carry):
        start = pl.multiple_of(j * K_TILE, K_TILE)
        k = k_ref[pl.ds(start, K_TILE), :]
        vt = vt_ref[j]
        k_doc = k_doc_ref[pl.ds(start, K_TILE), :]
        k_row = start + lax.broadcasted_iota(jnp.int32, (K_TILE, 1), 0)
        bias = jnp.where((k_doc == q_doc) & (k_row <= q_col), 0.0, NEG_FILL)
        for h in range(heads):
            q = q_ref[:, h * HEAD_SIZE:(h + 1) * HEAD_SIZE]
            scores = lax.dot_general(
                k, q, (((1,), (1,)), ((), ())), preferred_element_type=jnp.float32
            ) + bias
            peak = peak_sc[h]
            new_peak = jnp.maximum(peak, jnp.max(scores, axis=0, keepdims=True))
            floor = jnp.maximum(new_peak, 0.1 * NEG_FILL)
            weights = jnp.exp2((scores - floor) * rate)
            factor = jnp.exp2((peak - new_peak) * rate)
            total_sc[h] = total_sc[h] * factor + jnp.sum(weights, axis=0, keepdims=True)
            summed_sc[h] = summed_sc[h] * factor + jnp.dot(
                vt, weights.astype(jnp.bfloat16), preferred_element_type=jnp.float32
            )
            peak_sc[h] = new_peak
        return carry

    lax.fori_loop(lo, hi + 1, body, 0)
    for h in range(heads):
        o_ref[:, h * HEAD_SIZE:(h + 1) * HEAD_SIZE] = (
            (summed_sc[h] / total_sc[h]).T
        ).astype(o_ref.dtype)


def attend(bounds, q_doc, q_col, k_doc, q2, k_ext, vt_ext, heads, ext_off):
    rows = q2.shape[0]
    ext = k_ext.shape[0]
    n_q = rows // Q_TILE
    n_k = ext // K_TILE
    kernel = functools.partial(attend_kernel, heads=heads, ext_off=ext_off)
    grid_spec = pltpu.PrefetchScalarGridSpec(
        num_scalar_prefetch=1,
        grid=(n_q,),
        in_specs=[
            pl.BlockSpec((1, Q_TILE), lambda i, b: (0, i)),
            pl.BlockSpec((1, Q_TILE), lambda i, b: (0, i)),
            pl.BlockSpec((ext, 1), lambda i, b: (0, 0)),
            pl.BlockSpec((Q_TILE, heads * HEAD_SIZE), lambda i, b: (i, 0)),
            pl.BlockSpec((ext, HEAD_SIZE), lambda i, b: (0, 0)),
            pl.BlockSpec((n_k, HEAD_SIZE, K_TILE), lambda i, b: (0, 0, 0)),
        ],
        out_specs=pl.BlockSpec((Q_TILE, heads * HEAD_SIZE), lambda i, b: (i, 0)),
        scratch_shapes=[
            pltpu.VMEM((heads, 1, Q_TILE), jnp.float32),
            pltpu.VMEM((heads, 1, Q_TILE), jnp.float32),
            pltpu.VMEM((heads, HEAD_SIZE, Q_TILE), jnp.float32),
        ],
    )
    return pl.pallas_call(
        kernel,
        grid_spec=grid_spec,
        out_shape=jax.ShapeDtypeStruct((rows, heads * HEAD_SIZE), jnp.bfloat16),
        compiler_params=pltpu.CompilerParams(),
    )(bounds, q_doc, q_col, k_doc, q2, k_ext, vt_ext)


def tile_bounds(position, block, ext_off, ext, doc_lengths, local):
    ends = jnp.cumsum(doc_lengths)
    starts = ends - doc_lengths
    n_k = ext // K_TILE
    tiles = local.reshape(-1, Q_TILE)
    first = position * block + tiles[:, 0]
    first_doc = jnp.clip(doc_index(first, doc_lengths), 0, doc_lengths.shape[0] - 1)
    lo_key = starts[first_doc] - position * block + ext_off
    lo_key = jnp.maximum(lo_key, 0)
    hi_key = tiles[:, -1] + ext_off
    hi = jnp.clip(hi_key // K_TILE, 0, n_k - 1)
    lo = jnp.clip(lo_key // K_TILE, 0, hi)
    return jnp.stack([lo, hi], axis=1).reshape(-1).astype(jnp.int32)


def per_device(queries, keys, values, doc_lengths):
    token_rows = queries.shape[0]
    kv_heads = jnp.stack(
        [
            keys.reshape(token_rows, KEY_VALUE_HEADS, HEAD_SIZE),
            values.reshape(token_rows, KEY_VALUE_HEADS, HEAD_SIZE),
        ],
        axis=2,
    )
    kv_local = lax.all_to_all(kv_heads, "uly", split_axis=1, concat_axis=0, tiled=True)
    block = kv_local.shape[0]
    ext_off = CYCLE * block
    ext = ext_off + block
    position = lax.axis_index("blk")
    n_uly = block // token_rows

    pieces = [kv_local]
    for back in range(1, CYCLE + 1):
        pieces.append(passed_along(kv_local, "blk", back))
    kv_ext = jnp.concatenate(pieces[::-1], axis=0)
    k_ext = kv_ext[:, 0, 0, :]
    v_ext = kv_ext[:, 0, 1, :]
    vt_ext = v_ext.reshape(ext // K_TILE, K_TILE, HEAD_SIZE).transpose(0, 2, 1)
    k_pos = position * block - ext_off + jnp.arange(ext, dtype=jnp.int32)
    k_doc = jnp.where(k_pos >= 0, doc_index(k_pos, doc_lengths), -1)
    k_doc = k_doc.reshape(ext, 1)

    rows = token_rows // SPLITS
    outs = []
    for part in range(SPLITS):
        q_part = queries[part * rows:(part + 1) * rows].reshape(rows, QUERY_HEADS, HEAD_SIZE)
        q_local = lax.all_to_all(q_part, "uly", split_axis=1, concat_axis=0, tiled=True)
        heads = q_local.shape[1]
        chunk = jnp.arange(n_uly, dtype=jnp.int32)[:, None] * token_rows
        local = (chunk + part * rows + jnp.arange(rows, dtype=jnp.int32)[None, :]).reshape(-1)
        q_doc = doc_index(position * block + local, doc_lengths).reshape(1, -1)
        q_col = (local + ext_off).reshape(1, -1)
        bounds = tile_bounds(position, block, ext_off, ext, doc_lengths, local)
        q2 = q_local.reshape(-1, heads * HEAD_SIZE)
        result = attend(bounds, q_doc, q_col, k_doc, q2, k_ext, vt_ext, heads, ext_off)
        result = result.reshape(-1, heads, HEAD_SIZE)
        outs.append(lax.all_to_all(result, "uly", split_axis=0, concat_axis=1, tiled=True))
    returned = jnp.concatenate(outs, axis=0)
    return returned.reshape(token_rows, QUERY_HEADS * HEAD_SIZE)


def solution(mesh):
    in_specs = (
        P(("dp", "blk", "uly"), None),
        P(("dp", "blk", "uly"), None),
        P(("dp", "blk", "uly"), None),
        P("dp"),
    )
    out_specs = P(("dp", "blk", "uly"), None)
    return jax.shard_map(
        per_device, mesh=mesh, in_specs=in_specs, out_specs=out_specs, check_vma=False
    )
```

```python
import functools
import math

import jax
import jax.numpy as jnp
from jax import lax
from jax.experimental import pallas as pl
from jax.experimental.pallas import tpu as pltpu
from jax.sharding import PartitionSpec as P

QUERY_HEADS = 32
KEY_VALUE_HEADS = 8
HEAD_SIZE = 128
CYCLE = 2

Q_TILE = 128
K_TILE = 512

NEG_FILL = -1e30


def passed_along(block, axis, distance):
    devices = range(lax.axis_size(axis))
    route = [(i - distance, i) for i in devices if i - distance in devices]
    return lax.ppermute(block, axis, route)


def doc_index(positions, doc_lengths):
    ends = jnp.cumsum(doc_lengths)
    return jnp.sum((positions[:, None] >= ends[None, :]).astype(jnp.int32), axis=1)


def attend_kernel(bounds_ref, q_doc_ref, k_doc_ref, q_ref, k_ref, vt_ref, o_ref,
                  peak_sc, total_sc, summed_sc, *, heads, ext_off):
    i = pl.program_id(0)
    lo = bounds_ref[4 * i]
    mid_lo = bounds_ref[4 * i + 1]
    mid_hi = bounds_ref[4 * i + 2]
    hi = bounds_ref[4 * i + 3]
    peak_sc[...] = jnp.full(peak_sc.shape, NEG_FILL, jnp.float32)
    total_sc[...] = jnp.zeros(total_sc.shape, jnp.float32)
    summed_sc[...] = jnp.zeros(summed_sc.shape, jnp.float32)
    q_doc = q_doc_ref[...]
    q_col = i * Q_TILE + ext_off + lax.broadcasted_iota(jnp.int32, (1, Q_TILE), 1)
    rate = math.log2(math.e) / math.sqrt(HEAD_SIZE)

    def step(j, masked):
        start = pl.multiple_of(j * K_TILE, K_TILE)
        k = k_ref[pl.ds(start, K_TILE), :]
        vt = vt_ref[j]
        if masked:
            k_doc = k_doc_ref[pl.ds(start, K_TILE), :]
            k_row = start + lax.broadcasted_iota(jnp.int32, (K_TILE, 1), 0)
            bias = jnp.where((k_doc == q_doc) & (k_row <= q_col), 0.0, NEG_FILL)
        for h in range(heads):
            q = q_ref[:, h * HEAD_SIZE:(h + 1) * HEAD_SIZE]
            scores = lax.dot_general(
                k, q, (((1,), (1,)), ((), ())), preferred_element_type=jnp.float32
            )
            if masked:
                scores = scores + bias
            peak = peak_sc[h]
            new_peak = jnp.maximum(peak, jnp.max(scores, axis=0, keepdims=True))
            floor = jnp.maximum(new_peak, 0.1 * NEG_FILL) if masked else new_peak
            weights = jnp.exp2((scores - floor) * rate)
            factor = jnp.exp2((peak - new_peak) * rate)
            total_sc[h] = total_sc[h] * factor + jnp.sum(weights, axis=0, keepdims=True)
            summed_sc[h] = summed_sc[h] * factor + jnp.dot(
                vt, weights.astype(jnp.bfloat16), preferred_element_type=jnp.float32
            )
            peak_sc[h] = new_peak

    def masked_step(j, carry):
        step(j, True)
        return carry

    def open_step(j, carry):
        step(j, False)
        return carry

    lax.fori_loop(mid_lo, mid_hi, open_step, 0)
    lax.fori_loop(lo, mid_lo, masked_step, 0)
    lax.fori_loop(mid_hi, hi, masked_step, 0)
    for h in range(heads):
        o_ref[:, h * HEAD_SIZE:(h + 1) * HEAD_SIZE] = (
            (summed_sc[h] / total_sc[h]).T
        ).astype(o_ref.dtype)


def attend(bounds, q_doc, k_doc, q2, k_ext, vt_ext, heads, ext_off):
    rows = q2.shape[0]
    ext = k_ext.shape[0]
    n_q = rows // Q_TILE
    n_k = ext // K_TILE
    kernel = functools.partial(attend_kernel, heads=heads, ext_off=ext_off)
    grid_spec = pltpu.PrefetchScalarGridSpec(
        num_scalar_prefetch=1,
        grid=(n_q,),
        in_specs=[
            pl.BlockSpec((1, Q_TILE), lambda i, b: (0, i)),
            pl.BlockSpec((ext, 1), lambda i, b: (0, 0)),
            pl.BlockSpec((Q_TILE, heads * HEAD_SIZE), lambda i, b: (i, 0)),
            pl.BlockSpec((ext, HEAD_SIZE), lambda i, b: (0, 0)),
            pl.BlockSpec((n_k, HEAD_SIZE, K_TILE), lambda i, b: (0, 0, 0)),
        ],
        out_specs=pl.BlockSpec((Q_TILE, heads * HEAD_SIZE), lambda i, b: (i, 0)),
        scratch_shapes=[
            pltpu.VMEM((heads, 1, Q_TILE), jnp.float32),
            pltpu.VMEM((heads, 1, Q_TILE), jnp.float32),
            pltpu.VMEM((heads, HEAD_SIZE, Q_TILE), jnp.float32),
        ],
    )
    return pl.pallas_call(
        kernel,
        grid_spec=grid_spec,
        out_shape=jax.ShapeDtypeStruct((rows, heads * HEAD_SIZE), jnp.bfloat16),
        compiler_params=pltpu.CompilerParams(),
    )(bounds, q_doc, k_doc, q2, k_ext, vt_ext)


def tile_bounds(position, block, ext_off, ext, doc_lengths):
    ends = jnp.cumsum(doc_lengths)
    starts = ends - doc_lengths
    n_q = block // Q_TILE
    n_k = ext // K_TILE
    first_local = jnp.arange(n_q, dtype=jnp.int32) * Q_TILE
    first = position * block + first_local
    last = first + Q_TILE - 1
    first_doc = jnp.clip(doc_index(first, doc_lengths), 0, doc_lengths.shape[0] - 1)
    last_doc = doc_index(last, doc_lengths)
    start_ext = starts[first_doc] - position * block + ext_off
    lo_key = jnp.maximum(start_ext, 0)
    hi_key = first_local + Q_TILE - 1 + ext_off
    hi = jnp.clip(hi_key // K_TILE, 0, n_k - 1)
    lo = jnp.clip(lo_key // K_TILE, 0, hi)
    open_lo = (lo_key + K_TILE - 1) // K_TILE
    open_hi = (first_local + ext_off + 1) // K_TILE
    open_lo = jnp.clip(open_lo, lo, hi + 1)
    open_hi = jnp.clip(open_hi, open_lo, hi + 1)
    same = (first_doc == last_doc) & (start_ext >= 0)
    open_lo = jnp.where(same, open_lo, lo)
    open_hi = jnp.where(same, open_hi, lo)
    return jnp.stack([lo, open_lo, open_hi, hi + 1], axis=1).reshape(-1).astype(jnp.int32)


def per_device(queries, keys, values, doc_lengths):
    token_rows = queries.shape[0]
    q_heads = queries.reshape(token_rows, QUERY_HEADS, HEAD_SIZE)
    kv_heads = jnp.stack(
        [
            keys.reshape(token_rows, KEY_VALUE_HEADS, HEAD_SIZE),
            values.reshape(token_rows, KEY_VALUE_HEADS, HEAD_SIZE),
        ],
        axis=2,
    )
    q_local, kv_local = (
        lax.all_to_all(q_heads, "uly", split_axis=1, concat_axis=0, tiled=True),
        lax.all_to_all(kv_heads, "uly", split_axis=1, concat_axis=0, tiled=True),
    )
    block = q_local.shape[0]
    heads = q_local.shape[1]
    ext_off = CYCLE * block
    ext = ext_off + block
    position = lax.axis_index("blk")

    pieces = [kv_local]
    for back in range(1, CYCLE + 1):
        pieces.append(passed_along(kv_local, "blk", back))
    kv_ext = jnp.concatenate(pieces[::-1], axis=0)
    k_ext = kv_ext[:, 0, 0, :]
    v_ext = kv_ext[:, 0, 1, :]

    q_pos = position * block + jnp.arange(block, dtype=jnp.int32)
    q_doc = doc_index(q_pos, doc_lengths).reshape(1, block)
    k_pos = position * block - ext_off + jnp.arange(ext, dtype=jnp.int32)
    k_doc = jnp.where(k_pos >= 0, doc_index(k_pos, doc_lengths), -1)
    k_doc = k_doc.reshape(ext, 1)
    bounds = tile_bounds(position, block, ext_off, ext, doc_lengths)

    q2 = q_local.reshape(block, heads * HEAD_SIZE)
    vt_ext = v_ext.reshape(ext // K_TILE, K_TILE, HEAD_SIZE).transpose(0, 2, 1)
    result = attend(bounds, q_doc, k_doc, q2, k_ext, vt_ext, heads, ext_off)
    result = result.reshape(block, heads, HEAD_SIZE)
    returned = lax.all_to_all(result, "uly", split_axis=0, concat_axis=1, tiled=True)
    return returned.reshape(token_rows, QUERY_HEADS * HEAD_SIZE)


def solution(mesh):
    in_specs = (
        P(("dp", "blk", "uly"), None),
        P(("dp", "blk", "uly"), None),
        P(("dp", "blk", "uly"), None),
        P("dp"),
    )
    out_specs = P(("dp", "blk", "uly"), None)
    return jax.shard_map(
        per_device, mesh=mesh, in_specs=in_specs, out_specs=out_specs, check_vma=False
    )
```

```python
import functools
import math

import jax
import jax.numpy as jnp
from jax import lax
from jax.experimental import pallas as pl
from jax.experimental.pallas import tpu as pltpu
from jax.sharding import PartitionSpec as P

QUERY_HEADS = 32
KEY_VALUE_HEADS = 8
HEAD_SIZE = 128
CYCLE = 2

Q_TILE = 128
K_TILE = 512

NEG_FILL = -1e30


def passed_along(block, axis, distance):
    devices = range(lax.axis_size(axis))
    route = [(i - distance, i) for i in devices if i - distance in devices]
    return lax.ppermute(block, axis, route)


def doc_index(positions, doc_lengths):
    ends = jnp.cumsum(doc_lengths)
    return jnp.sum((positions[:, None] >= ends[None, :]).astype(jnp.int32), axis=1)


def attend_kernel(bounds_ref, q_doc_ref, k_doc_ref, q_ref, k_ref, vt_ref, o_ref,
                  peak_sc, total_sc, summed_sc, *, heads, ext_off):
    i = pl.program_id(0)
    lo = bounds_ref[4 * i]
    mid_lo = bounds_ref[4 * i + 1]
    mid_hi = bounds_ref[4 * i + 2]
    hi = bounds_ref[4 * i + 3]
    peak_sc[...] = jnp.full(peak_sc.shape, NEG_FILL, jnp.float32)
    total_sc[...] = jnp.zeros(total_sc.shape, jnp.float32)
    summed_sc[...] = jnp.zeros(summed_sc.shape, jnp.float32)
    q_doc = q_doc_ref[...]
    q_col = i * Q_TILE + ext_off + lax.broadcasted_iota(jnp.int32, (1, Q_TILE), 1)
    rate = math.log2(math.e) / math.sqrt(HEAD_SIZE)

    def step(j, masked):
        start = pl.multiple_of(j * K_TILE, K_TILE)
        k = k_ref[pl.ds(start, K_TILE), :]
        vt = vt_ref[j]
        if masked:
            k_doc = k_doc_ref[pl.ds(start, K_TILE), :]
            k_row = start + lax.broadcasted_iota(jnp.int32, (K_TILE, 1), 0)
            bias = jnp.where((k_doc == q_doc) & (k_row <= q_col), 0.0, NEG_FILL)
        for h in range(heads):
            q = q_ref[:, h * HEAD_SIZE:(h + 1) * HEAD_SIZE]
            scores = lax.dot_general(
                k, q, (((1,), (1,)), ((), ())), preferred_element_type=jnp.float32
            )
            if masked:
                scores = scores + bias
            peak = peak_sc[h]
            new_peak = jnp.maximum(peak, jnp.max(scores, axis=0, keepdims=True))
            floor = jnp.maximum(new_peak, 0.1 * NEG_FILL) if masked else new_peak
            weights = jnp.exp2((scores - floor) * rate)
            factor = jnp.exp2((peak - new_peak) * rate)
            total_sc[h] = total_sc[h] * factor + jnp.sum(weights, axis=0, keepdims=True)
            summed_sc[h] = summed_sc[h] * factor + jnp.dot(
                vt, weights.astype(jnp.bfloat16), preferred_element_type=jnp.float32
            )
            peak_sc[h] = new_peak

    def masked_step(j, carry):
        step(j, True)
        return carry

    def open_step(j, carry):
        step(j, False)
        return carry

    lax.fori_loop(mid_lo, mid_hi, open_step, 0)
    lax.fori_loop(lo, mid_lo, masked_step, 0)
    lax.fori_loop(mid_hi, hi, masked_step, 0)
    for h in range(heads):
        o_ref[:, h * HEAD_SIZE:(h + 1) * HEAD_SIZE] = (
            (summed_sc[h] / total_sc[h]).T
        ).astype(o_ref.dtype)


def attend(bounds, q_doc, k_doc, q2, k_ext, vt_ext, heads, ext_off):
    rows = q2.shape[0]
    ext = k_ext.shape[0]
    n_q = rows // Q_TILE
    n_k = ext // K_TILE
    kernel = functools.partial(attend_kernel, heads=heads, ext_off=ext_off)
    grid_spec = pltpu.PrefetchScalarGridSpec(
        num_scalar_prefetch=1,
        grid=(n_q,),
        in_specs=[
            pl.BlockSpec((1, Q_TILE), lambda i, b: (0, i)),
            pl.BlockSpec((ext, 1), lambda i, b: (0, 0)),
            pl.BlockSpec((Q_TILE, heads * HEAD_SIZE), lambda i, b: (i, 0)),
            pl.BlockSpec((ext, HEAD_SIZE), lambda i, b: (0, 0)),
            pl.BlockSpec((n_k, HEAD_SIZE, K_TILE), lambda i, b: (0, 0, 0)),
        ],
        out_specs=pl.BlockSpec((Q_TILE, heads * HEAD_SIZE), lambda i, b: (i, 0)),
        scratch_shapes=[
            pltpu.VMEM((heads, 1, Q_TILE), jnp.float32),
            pltpu.VMEM((heads, 1, Q_TILE), jnp.float32),
            pltpu.VMEM((heads, HEAD_SIZE, Q_TILE), jnp.float32),
        ],
    )
    return pl.pallas_call(
        kernel,
        grid_spec=grid_spec,
        out_shape=jax.ShapeDtypeStruct((rows, heads * HEAD_SIZE), jnp.bfloat16),
        compiler_params=pltpu.CompilerParams(),
    )(bounds, q_doc, k_doc, q2, k_ext, vt_ext)


def tile_bounds(position, block, ext_off, ext, doc_lengths):
    ends = jnp.cumsum(doc_lengths)
    starts = ends - doc_lengths
    n_q = block // Q_TILE
    n_k = ext // K_TILE
    first_local = jnp.arange(n_q, dtype=jnp.int32) * Q_TILE
    first = position * block + first_local
    last = first + Q_TILE - 1
    first_doc = jnp.clip(doc_index(first, doc_lengths), 0, doc_lengths.shape[0] - 1)
    last_doc = doc_index(last, doc_lengths)
    start_ext = starts[first_doc] - position * block + ext_off
    lo_key = jnp.maximum(start_ext, 0)
    hi_key = first_local + Q_TILE - 1 + ext_off
    hi = jnp.clip(hi_key // K_TILE, 0, n_k - 1)
    lo = jnp.clip(lo_key // K_TILE, 0, hi)
    open_lo = (lo_key + K_TILE - 1) // K_TILE
    open_hi = (first_local + ext_off + 1) // K_TILE
    open_lo = jnp.clip(open_lo, lo, hi + 1)
    open_hi = jnp.clip(open_hi, open_lo, hi + 1)
    same = (first_doc == last_doc) & (start_ext >= 0)
    open_lo = jnp.where(same, open_lo, lo)
    open_hi = jnp.where(same, open_hi, lo)
    return jnp.stack([lo, open_lo, open_hi, hi + 1], axis=1).reshape(-1).astype(jnp.int32)


def per_device(queries, keys, values, doc_lengths):
    token_rows = queries.shape[0]
    kv_heads = jnp.stack(
        [
            keys.reshape(token_rows, KEY_VALUE_HEADS, HEAD_SIZE),
            values.reshape(token_rows, KEY_VALUE_HEADS, HEAD_SIZE),
        ],
        axis=2,
    )
    n_uly = lax.axis_size("uly")
    heads = QUERY_HEADS // n_uly
    columns = heads * HEAD_SIZE
    q_dest = queries.reshape(token_rows, n_uly, columns).transpose(1, 0, 2)
    q_local, kv_local = (
        lax.all_to_all(q_dest, "uly", split_axis=0, concat_axis=0, tiled=True),
        lax.all_to_all(kv_heads, "uly", split_axis=1, concat_axis=0, tiled=True),
    )
    block = token_rows * n_uly
    ext_off = CYCLE * block
    ext = ext_off + block
    position = lax.axis_index("blk")

    pieces = [kv_local]
    for back in range(1, CYCLE + 1):
        pieces.append(passed_along(kv_local, "blk", back))
    kv_ext = jnp.concatenate(pieces[::-1], axis=0)
    k_ext = kv_ext[:, 0, 0, :]
    v_ext = kv_ext[:, 0, 1, :]

    q_pos = position * block + jnp.arange(block, dtype=jnp.int32)
    q_doc = doc_index(q_pos, doc_lengths).reshape(1, block)
    k_pos = position * block - ext_off + jnp.arange(ext, dtype=jnp.int32)
    k_doc = jnp.where(k_pos >= 0, doc_index(k_pos, doc_lengths), -1)
    k_doc = k_doc.reshape(ext, 1)
    bounds = tile_bounds(position, block, ext_off, ext, doc_lengths)

    q2 = q_local.reshape(block, columns)
    vt_ext = v_ext.reshape(ext // K_TILE, K_TILE, HEAD_SIZE).transpose(0, 2, 1)
    result = attend(bounds, q_doc, k_doc, q2, k_ext, vt_ext, heads, ext_off)
    result = result.reshape(n_uly, token_rows, columns)
    returned = lax.all_to_all(result, "uly", split_axis=0, concat_axis=0, tiled=True)
    return returned.transpose(1, 0, 2).reshape(token_rows, QUERY_HEADS * HEAD_SIZE)


def solution(mesh):
    in_specs = (
        P(("dp", "blk", "uly"), None),
        P(("dp", "blk", "uly"), None),
        P(("dp", "blk", "uly"), None),
        P("dp"),
    )
    out_specs = P(("dp", "blk", "uly"), None)
    return jax.shard_map(
        per_device, mesh=mesh, in_specs=in_specs, out_specs=out_specs, check_vma=False
    )
```

```python
import functools
import math

import jax
import jax.numpy as jnp
from jax import lax
from jax.experimental import pallas as pl
from jax.experimental.pallas import tpu as pltpu
from jax.sharding import PartitionSpec as P

QUERY_HEADS = 32
KEY_VALUE_HEADS = 8
HEAD_SIZE = 128
CYCLE = 2

Q_TILE = 128
K_TILE = 512

NEG_FILL = -1e30


def passed_along(block, axis, distance):
    devices = range(lax.axis_size(axis))
    route = [(i - distance, i) for i in devices if i - distance in devices]
    return lax.ppermute(block, axis, route)


def doc_index(positions, doc_lengths):
    ends = jnp.cumsum(doc_lengths)
    return jnp.sum((positions[:, None] >= ends[None, :]).astype(jnp.int32), axis=1)


def attend_kernel(bounds_ref, q_start_ref, q_ref, b2_ref, b1_ref, own_ref, o_ref,
                  k_sc, vt_sc, peak_sc, total_sc, summed_sc, *, heads, ext_off):
    i = pl.program_id(0)
    block = own_ref.shape[0]
    per_block = block // K_TILE

    @pl.when(i == 0)
    def _():
        for p, ref in enumerate((b2_ref, b1_ref, own_ref)):
            k_sc[p * block:(p + 1) * block, :] = ref[:, :HEAD_SIZE]
            for t in range(per_block):
                v = ref[t * K_TILE:(t + 1) * K_TILE, HEAD_SIZE:].astype(jnp.float32)
                vt_sc[p * per_block + t] = v.T.astype(vt_sc.dtype)

    lo = bounds_ref[4 * i]
    mid_lo = bounds_ref[4 * i + 1]
    mid_hi = bounds_ref[4 * i + 2]
    hi = bounds_ref[4 * i + 3]
    peak_sc[...] = jnp.full(peak_sc.shape, NEG_FILL, jnp.float32)
    total_sc[...] = jnp.zeros(total_sc.shape, jnp.float32)
    summed_sc[...] = jnp.zeros(summed_sc.shape, jnp.float32)
    q_start = q_start_ref[...]
    q_col = i * Q_TILE + ext_off + lax.broadcasted_iota(jnp.int32, (1, Q_TILE), 1)
    rate = math.log2(math.e) / math.sqrt(HEAD_SIZE)

    def step(j, masked):
        start = pl.multiple_of(j * K_TILE, K_TILE)
        k = k_sc[pl.ds(start, K_TILE), :]
        vt = vt_sc[j]
        if masked:
            k_row = start + lax.broadcasted_iota(jnp.int32, (K_TILE, 1), 0)
            bias = jnp.where((k_row >= q_start) & (k_row <= q_col), 0.0, NEG_FILL)
        for h in range(heads):
            q = q_ref[:, h * HEAD_SIZE:(h + 1) * HEAD_SIZE]
            scores = lax.dot_general(
                k, q, (((1,), (1,)), ((), ())), preferred_element_type=jnp.float32
            )
            if masked:
                scores = scores + bias
            peak = peak_sc[h]
            new_peak = jnp.maximum(peak, jnp.max(scores, axis=0, keepdims=True))
            floor = jnp.maximum(new_peak, 0.1 * NEG_FILL) if masked else new_peak
            weights = jnp.exp2((scores - floor) * rate)
            factor = jnp.exp2((peak - new_peak) * rate)
            total_sc[h] = total_sc[h] * factor + jnp.sum(weights, axis=0, keepdims=True)
            summed_sc[h] = summed_sc[h] * factor + jnp.dot(
                vt, weights.astype(jnp.bfloat16), preferred_element_type=jnp.float32
            )
            peak_sc[h] = new_peak

    def masked_step(j, carry):
        step(j, True)
        return carry

    def open_step(j, carry):
        step(j, False)
        return carry

    lax.fori_loop(mid_lo, mid_hi, open_step, 0)
    lax.fori_loop(lo, mid_lo, masked_step, 0)
    lax.fori_loop(mid_hi, hi, masked_step, 0)
    for h in range(heads):
        o_ref[:, h * HEAD_SIZE:(h + 1) * HEAD_SIZE] = (
            (summed_sc[h] / total_sc[h]).T
        ).astype(o_ref.dtype)


def attend(bounds, q_start, q2, kv_pieces, heads, ext_off):
    rows = q2.shape[0]
    block = kv_pieces[0].shape[0]
    ext = block * len(kv_pieces)
    n_q = rows // Q_TILE
    n_k = ext // K_TILE
    kernel = functools.partial(attend_kernel, heads=heads, ext_off=ext_off)
    kv_spec = pl.BlockSpec((block, 2 * HEAD_SIZE), lambda i, b: (0, 0))
    grid_spec = pltpu.PrefetchScalarGridSpec(
        num_scalar_prefetch=1,
        grid=(n_q,),
        in_specs=[
            pl.BlockSpec((1, Q_TILE), lambda i, b: (0, i)),
            pl.BlockSpec((Q_TILE, heads * HEAD_SIZE), lambda i, b: (i, 0)),
            kv_spec,
            kv_spec,
            kv_spec,
        ],
        out_specs=pl.BlockSpec((Q_TILE, heads * HEAD_SIZE), lambda i, b: (i, 0)),
        scratch_shapes=[
            pltpu.VMEM((ext, HEAD_SIZE), jnp.bfloat16),
            pltpu.VMEM((n_k, HEAD_SIZE, K_TILE), jnp.bfloat16),
            pltpu.VMEM((heads, 1, Q_TILE), jnp.float32),
            pltpu.VMEM((heads, 1, Q_TILE), jnp.float32),
            pltpu.VMEM((heads, HEAD_SIZE, Q_TILE), jnp.float32),
        ],
    )
    return pl.pallas_call(
        kernel,
        grid_spec=grid_spec,
        out_shape=jax.ShapeDtypeStruct((rows, heads * HEAD_SIZE), jnp.bfloat16),
        compiler_params=pltpu.CompilerParams(),
    )(bounds, q_start, q2, *kv_pieces)


def tile_bounds(position, block, ext_off, ext, doc_lengths):
    ends = jnp.cumsum(doc_lengths)
    starts = ends - doc_lengths
    n_q = block // Q_TILE
    n_k = ext // K_TILE
    first_local = jnp.arange(n_q, dtype=jnp.int32) * Q_TILE
    first = position * block + first_local
    last = first + Q_TILE - 1
    first_doc = jnp.clip(doc_index(first, doc_lengths), 0, doc_lengths.shape[0] - 1)
    last_doc = doc_index(last, doc_lengths)
    start_ext = starts[first_doc] - position * block + ext_off
    lo_key = jnp.maximum(start_ext, 0)
    hi_key = first_local + Q_TILE - 1 + ext_off
    hi = jnp.clip(hi_key // K_TILE, 0, n_k - 1)
    lo = jnp.clip(lo_key // K_TILE, 0, hi)
    open_lo = (lo_key + K_TILE - 1) // K_TILE
    open_hi = (first_local + ext_off + 1) // K_TILE
    open_lo = jnp.clip(open_lo, lo, hi + 1)
    open_hi = jnp.clip(open_hi, open_lo, hi + 1)
    same = (first_doc == last_doc) & (start_ext >= 0)
    open_lo = jnp.where(same, open_lo, lo)
    open_hi = jnp.where(same, open_hi, lo)
    return jnp.stack([lo, open_lo, open_hi, hi + 1], axis=1).reshape(-1).astype(jnp.int32)


def per_device(queries, keys, values, doc_lengths):
    token_rows = queries.shape[0]
    n_uly = lax.axis_size("uly")
    heads = QUERY_HEADS // n_uly
    columns = heads * HEAD_SIZE
    kv_columns = KEY_VALUE_HEADS * HEAD_SIZE // n_uly
    q_dest = queries.reshape(token_rows, n_uly, columns).transpose(1, 0, 2)
    kv_dest = jnp.concatenate(
        [
            keys.reshape(token_rows, n_uly, kv_columns),
            values.reshape(token_rows, n_uly, kv_columns),
        ],
        axis=2,
    ).transpose(1, 0, 2)
    kv_local = lax.all_to_all(kv_dest, "uly", split_axis=0, concat_axis=0, tiled=True)
    q_local = lax.all_to_all(q_dest, "uly", split_axis=0, concat_axis=0, tiled=True)
    block = token_rows * n_uly
    ext_off = CYCLE * block
    ext = ext_off + block
    position = lax.axis_index("blk")

    kv_local = kv_local.reshape(block, 2 * kv_columns)
    pieces = [kv_local]
    for back in range(1, CYCLE + 1):
        pieces.append(passed_along(kv_local, "blk", back))

    ends = jnp.cumsum(doc_lengths)
    starts = ends - doc_lengths
    q_pos = position * block + jnp.arange(block, dtype=jnp.int32)
    q_doc = jnp.clip(doc_index(q_pos, doc_lengths), 0, doc_lengths.shape[0] - 1)
    q_start = (starts[q_doc] - position * block + ext_off).reshape(1, block)
    bounds = tile_bounds(position, block, ext_off, ext, doc_lengths)

    q2 = q_local.reshape(block, columns)
    result = attend(bounds, q_start, q2, pieces[::-1], heads, ext_off)
    result = result.reshape(n_uly, token_rows, columns)
    returned = lax.all_to_all(result, "uly", split_axis=0, concat_axis=0, tiled=True)
    return returned.transpose(1, 0, 2).reshape(token_rows, QUERY_HEADS * HEAD_SIZE)


def solution(mesh):
    in_specs = (
        P(("dp", "blk", "uly"), None),
        P(("dp", "blk", "uly"), None),
        P(("dp", "blk", "uly"), None),
        P("dp"),
    )
    out_specs = P(("dp", "blk", "uly"), None)
    return jax.shard_map(
        per_device, mesh=mesh, in_specs=in_specs, out_specs=out_specs, check_vma=False
    )
```

```python
import functools
import math

import jax
import jax.numpy as jnp
from jax import lax
from jax.experimental import pallas as pl
from jax.experimental.pallas import tpu as pltpu
from jax.sharding import PartitionSpec as P

QUERY_HEADS = 32
KEY_VALUE_HEADS = 8
HEAD_SIZE = 128
CYCLE = 2

Q_TILE = 128
K_TILE = 512

NEG_FILL = -1e30


def passed_along(block, axis, distance):
    devices = range(lax.axis_size(axis))
    route = [(i - distance, i) for i in devices if i - distance in devices]
    return lax.ppermute(block, axis, route)


def doc_index(positions, doc_lengths):
    ends = jnp.cumsum(doc_lengths)
    return jnp.sum((positions[:, None] >= ends[None, :]).astype(jnp.int32), axis=1)


def attend_kernel(bounds_ref, q_start_ref, q_ref, b2_ref, b1_ref, own_ref, o_ref,
                  k_sc, vt_sc, peak_sc, total_sc, summed_sc, *, heads, ext_off):
    i = pl.program_id(0)
    block = own_ref.shape[0]
    per_block = block // K_TILE

    @pl.when(i == 0)
    def _():
        for p, ref in enumerate((b2_ref, b1_ref, own_ref)):
            k_sc[p * block:(p + 1) * block, :] = ref[:, :HEAD_SIZE]
            for t in range(per_block):
                v = ref[t * K_TILE:(t + 1) * K_TILE, HEAD_SIZE:].astype(jnp.float32)
                vt_sc[p * per_block + t] = v.T.astype(vt_sc.dtype)

    lo = bounds_ref[4 * i]
    mid_lo = bounds_ref[4 * i + 1]
    mid_hi = bounds_ref[4 * i + 2]
    hi = bounds_ref[4 * i + 3]
    peak_sc[...] = jnp.full(peak_sc.shape, NEG_FILL, jnp.float32)
    total_sc[...] = jnp.zeros(total_sc.shape, jnp.float32)
    summed_sc[...] = jnp.zeros(summed_sc.shape, jnp.float32)
    q_start = q_start_ref[...]
    q_col = i * Q_TILE + ext_off + lax.broadcasted_iota(jnp.int32, (1, Q_TILE), 1)
    rate = math.log2(math.e) / math.sqrt(HEAD_SIZE)

    def step(j, masked):
        start = pl.multiple_of(j * K_TILE, K_TILE)
        k = k_sc[pl.ds(start, K_TILE), :]
        vt = vt_sc[j]
        if masked:
            k_row = start + lax.broadcasted_iota(jnp.int32, (K_TILE, 1), 0)
            bias = jnp.where((k_row >= q_start) & (k_row <= q_col), 0.0, NEG_FILL)
        for h in range(heads):
            q = q_ref[:, h * HEAD_SIZE:(h + 1) * HEAD_SIZE]
            scores = lax.dot_general(
                k, q, (((1,), (1,)), ((), ())), preferred_element_type=jnp.float32
            )
            if masked:
                scores = scores + bias
            peak = peak_sc[h]
            new_peak = jnp.maximum(peak, jnp.max(scores, axis=0, keepdims=True))
            floor = jnp.maximum(new_peak, 0.1 * NEG_FILL) if masked else new_peak
            weights = jnp.exp2((scores - floor) * rate)
            factor = jnp.exp2((peak - new_peak) * rate)
            total_sc[h] = total_sc[h] * factor + jnp.sum(weights, axis=0, keepdims=True)
            summed_sc[h] = summed_sc[h] * factor + jnp.dot(
                vt, weights.astype(jnp.bfloat16), preferred_element_type=jnp.float32
            )
            peak_sc[h] = new_peak

    def masked_step(j, carry):
        step(j, True)
        return carry

    def open_step(j, carry):
        step(j, False)
        return carry

    lax.fori_loop(mid_lo, mid_hi, open_step, 0)
    lax.fori_loop(lo, mid_lo, masked_step, 0)
    lax.fori_loop(mid_hi, hi, masked_step, 0)
    for h in range(heads):
        o_ref[:, h * HEAD_SIZE:(h + 1) * HEAD_SIZE] = (
            (summed_sc[h] / total_sc[h]).T
        ).astype(o_ref.dtype)


def attend(bounds, q_start, q2, kv_pieces, heads, ext_off):
    rows = q2.shape[0]
    block = kv_pieces[0].shape[0]
    ext = block * len(kv_pieces)
    n_q = rows // Q_TILE
    n_k = ext // K_TILE
    kernel = functools.partial(attend_kernel, heads=heads, ext_off=ext_off)
    kv_spec = pl.BlockSpec((block, 2 * HEAD_SIZE), lambda i, b: (0, 0))
    grid_spec = pltpu.PrefetchScalarGridSpec(
        num_scalar_prefetch=1,
        grid=(n_q,),
        in_specs=[
            pl.BlockSpec((1, Q_TILE), lambda i, b: (0, i)),
            pl.BlockSpec((Q_TILE, heads * HEAD_SIZE), lambda i, b: (i, 0)),
            kv_spec,
            kv_spec,
            kv_spec,
        ],
        out_specs=pl.BlockSpec((Q_TILE, heads * HEAD_SIZE), lambda i, b: (i, 0)),
        scratch_shapes=[
            pltpu.VMEM((ext, HEAD_SIZE), jnp.bfloat16),
            pltpu.VMEM((n_k, HEAD_SIZE, K_TILE), jnp.bfloat16),
            pltpu.VMEM((heads, 1, Q_TILE), jnp.float32),
            pltpu.VMEM((heads, 1, Q_TILE), jnp.float32),
            pltpu.VMEM((heads, HEAD_SIZE, Q_TILE), jnp.float32),
        ],
    )
    return pl.pallas_call(
        kernel,
        grid_spec=grid_spec,
        out_shape=jax.ShapeDtypeStruct((rows, heads * HEAD_SIZE), jnp.bfloat16),
        compiler_params=pltpu.CompilerParams(),
    )(bounds, q_start, q2, *kv_pieces)


def doc_start(positions, doc_lengths):
    ends = jnp.cumsum(doc_lengths)
    return jnp.max(jnp.where(ends[None, :] <= positions[:, None], ends[None, :], 0), axis=1)


def tile_bounds(position, block, ext_off, ext, doc_lengths):
    n_q = block // Q_TILE
    n_k = ext // K_TILE
    first_local = jnp.arange(n_q, dtype=jnp.int32) * Q_TILE
    first = position * block + first_local
    last = first + Q_TILE - 1
    first_start = doc_start(first, doc_lengths)
    last_start = doc_start(last, doc_lengths)
    start_ext = first_start - position * block + ext_off
    lo_key = jnp.maximum(start_ext, 0)
    hi_key = first_local + Q_TILE - 1 + ext_off
    hi = jnp.clip(hi_key // K_TILE, 0, n_k - 1)
    lo = jnp.clip(lo_key // K_TILE, 0, hi)
    open_lo = (lo_key + K_TILE - 1) // K_TILE
    open_hi = (first_local + ext_off + 1) // K_TILE
    open_lo = jnp.clip(open_lo, lo, hi + 1)
    open_hi = jnp.clip(open_hi, open_lo, hi + 1)
    same = (first_start == last_start) & (start_ext >= 0)
    open_lo = jnp.where(same, open_lo, lo)
    open_hi = jnp.where(same, open_hi, lo)
    return jnp.stack([lo, open_lo, open_hi, hi + 1], axis=1).reshape(-1).astype(jnp.int32)


def per_device(queries, keys, values, doc_lengths):
    token_rows = queries.shape[0]
    n_uly = lax.axis_size("uly")
    heads = QUERY_HEADS // n_uly
    columns = heads * HEAD_SIZE
    kv_columns = KEY_VALUE_HEADS * HEAD_SIZE // n_uly
    q_dest = queries.reshape(token_rows, n_uly, columns).transpose(1, 0, 2)
    kv_dest = jnp.concatenate(
        [
            keys.reshape(token_rows, n_uly, kv_columns),
            values.reshape(token_rows, n_uly, kv_columns),
        ],
        axis=2,
    ).transpose(1, 0, 2)
    kv_local = lax.all_to_all(kv_dest, "uly", split_axis=0, concat_axis=0, tiled=True)
    q_local = lax.all_to_all(q_dest, "uly", split_axis=0, concat_axis=0, tiled=True)
    block = token_rows * n_uly
    ext_off = CYCLE * block
    ext = ext_off + block
    position = lax.axis_index("blk")

    kv_local = kv_local.reshape(block, 2 * kv_columns)
    pieces = [kv_local]
    for back in range(1, CYCLE + 1):
        pieces.append(passed_along(kv_local, "blk", back))

    q_pos = position * block + jnp.arange(block, dtype=jnp.int32)
    q_start = (doc_start(q_pos, doc_lengths) - position * block + ext_off).reshape(1, block)
    bounds = tile_bounds(position, block, ext_off, ext, doc_lengths)

    q2 = q_local.reshape(block, columns)
    result = attend(bounds, q_start, q2, pieces[::-1], heads, ext_off)
    result = result.reshape(n_uly, token_rows, columns)
    returned = lax.all_to_all(result, "uly", split_axis=0, concat_axis=0, tiled=True)
    return returned.transpose(1, 0, 2).reshape(token_rows, QUERY_HEADS * HEAD_SIZE)


def solution(mesh):
    in_specs = (
        P(("dp", "blk", "uly"), None),
        P(("dp", "blk", "uly"), None),
        P(("dp", "blk", "uly"), None),
        P("dp"),
    )
    out_specs = P(("dp", "blk", "uly"), None)
    return jax.shard_map(
        per_device, mesh=mesh, in_specs=in_specs, out_specs=out_specs, check_vma=False
    )
```

```python
import functools
import math

import jax
import jax.numpy as jnp
from jax import lax
from jax.experimental import pallas as pl
from jax.experimental.pallas import tpu as pltpu
from jax.sharding import PartitionSpec as P

QUERY_HEADS = 32
KEY_VALUE_HEADS = 8
HEAD_SIZE = 128
CYCLE = 2

Q_TILE = 128
K_TILE = 512
PER_STEP = 2

NEG_FILL = -1e30


def passed_along(block, axis, distance):
    devices = range(lax.axis_size(axis))
    route = [(i - distance, i) for i in devices if i - distance in devices]
    return lax.ppermute(block, axis, route)


def doc_index(positions, doc_lengths):
    ends = jnp.cumsum(doc_lengths)
    return jnp.sum((positions[:, None] >= ends[None, :]).astype(jnp.int32), axis=1)


def attend_kernel(bounds_ref, q_start_ref, q_ref, b2_ref, b1_ref, own_ref, o_ref,
                  k_sc, vt_sc, peak_sc, total_sc, summed_sc, *, heads, ext_off):
    i = pl.program_id(0)
    block = own_ref.shape[0]
    per_block = block // K_TILE

    @pl.when(i == 0)
    def _():
        for p, ref in enumerate((b2_ref, b1_ref, own_ref)):
            k_sc[p * block:(p + 1) * block, :] = ref[:, :HEAD_SIZE]
            for t in range(per_block):
                v = ref[t * K_TILE:(t + 1) * K_TILE, HEAD_SIZE:].astype(jnp.float32)
                vt_sc[p * per_block + t] = v.T.astype(vt_sc.dtype)

    rate = math.log2(math.e) / math.sqrt(HEAD_SIZE)
    for sub in range(PER_STEP):
        attend_tile(i * PER_STEP + sub, sub, bounds_ref, q_start_ref, q_ref, o_ref,
                    k_sc, vt_sc, peak_sc, total_sc, summed_sc, heads, ext_off, rate)


def attend_tile(t, sub, bounds_ref, q_start_ref, q_ref, o_ref,
                k_sc, vt_sc, peak_sc, total_sc, summed_sc, heads, ext_off, rate):
    rows = slice(sub * Q_TILE, (sub + 1) * Q_TILE)
    lo = bounds_ref[4 * t]
    mid_lo = bounds_ref[4 * t + 1]
    mid_hi = bounds_ref[4 * t + 2]
    hi = bounds_ref[4 * t + 3]
    peak_sc[...] = jnp.full(peak_sc.shape, NEG_FILL, jnp.float32)
    total_sc[...] = jnp.zeros(total_sc.shape, jnp.float32)
    summed_sc[...] = jnp.zeros(summed_sc.shape, jnp.float32)
    q_start = q_start_ref[:, rows]
    q_col = t * Q_TILE + ext_off + lax.broadcasted_iota(jnp.int32, (1, Q_TILE), 1)

    def step(j, masked):
        start = pl.multiple_of(j * K_TILE, K_TILE)
        k = k_sc[pl.ds(start, K_TILE), :]
        vt = vt_sc[j]
        if masked:
            k_row = start + lax.broadcasted_iota(jnp.int32, (K_TILE, 1), 0)
            bias = jnp.where((k_row >= q_start) & (k_row <= q_col), 0.0, NEG_FILL)
        for h in range(heads):
            q = q_ref[rows, h * HEAD_SIZE:(h + 1) * HEAD_SIZE]
            scores = lax.dot_general(
                k, q, (((1,), (1,)), ((), ())), preferred_element_type=jnp.float32
            )
            if masked:
                scores = scores + bias
            peak = peak_sc[h]
            new_peak = jnp.maximum(peak, jnp.max(scores, axis=0, keepdims=True))
            floor = jnp.maximum(new_peak, 0.1 * NEG_FILL) if masked else new_peak
            weights = jnp.exp2((scores - floor) * rate)
            factor = jnp.exp2((peak - new_peak) * rate)
            total_sc[h] = total_sc[h] * factor + jnp.sum(weights, axis=0, keepdims=True)
            summed_sc[h] = summed_sc[h] * factor + jnp.dot(
                vt, weights.astype(jnp.bfloat16), preferred_element_type=jnp.float32
            )
            peak_sc[h] = new_peak

    def masked_step(j, carry):
        step(j, True)
        return carry

    def open_step(j, carry):
        step(j, False)
        return carry

    lax.fori_loop(mid_lo, mid_hi, open_step, 0)
    lax.fori_loop(lo, mid_lo, masked_step, 0)
    lax.fori_loop(mid_hi, hi, masked_step, 0)
    for h in range(heads):
        o_ref[rows, h * HEAD_SIZE:(h + 1) * HEAD_SIZE] = (
            (summed_sc[h] / total_sc[h]).T
        ).astype(o_ref.dtype)


def attend(bounds, q_start, q2, kv_pieces, heads, ext_off):
    rows = q2.shape[0]
    block = kv_pieces[0].shape[0]
    ext = block * len(kv_pieces)
    n_q = rows // (Q_TILE * PER_STEP)
    n_k = ext // K_TILE
    kernel = functools.partial(attend_kernel, heads=heads, ext_off=ext_off)
    kv_spec = pl.BlockSpec((block, 2 * HEAD_SIZE), lambda i, b: (0, 0))
    grid_spec = pltpu.PrefetchScalarGridSpec(
        num_scalar_prefetch=1,
        grid=(n_q,),
        in_specs=[
            pl.BlockSpec((1, Q_TILE * PER_STEP), lambda i, b: (0, i)),
            pl.BlockSpec((Q_TILE * PER_STEP, heads * HEAD_SIZE), lambda i, b: (i, 0)),
            kv_spec,
            kv_spec,
            kv_spec,
        ],
        out_specs=pl.BlockSpec((Q_TILE * PER_STEP, heads * HEAD_SIZE), lambda i, b: (i, 0)),
        scratch_shapes=[
            pltpu.VMEM((ext, HEAD_SIZE), jnp.bfloat16),
            pltpu.VMEM((n_k, HEAD_SIZE, K_TILE), jnp.bfloat16),
            pltpu.VMEM((heads, 1, Q_TILE), jnp.float32),
            pltpu.VMEM((heads, 1, Q_TILE), jnp.float32),
            pltpu.VMEM((heads, HEAD_SIZE, Q_TILE), jnp.float32),
        ],
    )
    return pl.pallas_call(
        kernel,
        grid_spec=grid_spec,
        out_shape=jax.ShapeDtypeStruct((rows, heads * HEAD_SIZE), jnp.bfloat16),
        compiler_params=pltpu.CompilerParams(),
    )(bounds, q_start, q2, *kv_pieces)


def tile_bounds(position, block, ext_off, ext, doc_lengths):
    ends = jnp.cumsum(doc_lengths)
    starts = ends - doc_lengths
    n_q = block // Q_TILE
    n_k = ext // K_TILE
    first_local = jnp.arange(n_q, dtype=jnp.int32) * Q_TILE
    first = position * block + first_local
    last = first + Q_TILE - 1
    first_doc = jnp.clip(doc_index(first, doc_lengths), 0, doc_lengths.shape[0] - 1)
    last_doc = doc_index(last, doc_lengths)
    start_ext = starts[first_doc] - position * block + ext_off
    lo_key = jnp.maximum(start_ext, 0)
    hi_key = first_local + Q_TILE - 1 + ext_off
    hi = jnp.clip(hi_key // K_TILE, 0, n_k - 1)
    lo = jnp.clip(lo_key // K_TILE, 0, hi)
    open_lo = (lo_key + K_TILE - 1) // K_TILE
    open_hi = (first_local + ext_off + 1) // K_TILE
    open_lo = jnp.clip(open_lo, lo, hi + 1)
    open_hi = jnp.clip(open_hi, open_lo, hi + 1)
    same = (first_doc == last_doc) & (start_ext >= 0)
    open_lo = jnp.where(same, open_lo, lo)
    open_hi = jnp.where(same, open_hi, lo)
    return jnp.stack([lo, open_lo, open_hi, hi + 1], axis=1).reshape(-1).astype(jnp.int32)


def per_device(queries, keys, values, doc_lengths):
    token_rows = queries.shape[0]
    n_uly = lax.axis_size("uly")
    heads = QUERY_HEADS // n_uly
    columns = heads * HEAD_SIZE
    kv_columns = KEY_VALUE_HEADS * HEAD_SIZE // n_uly
    q_dest = queries.reshape(token_rows, n_uly, columns).transpose(1, 0, 2)
    kv_dest = jnp.concatenate(
        [
            keys.reshape(token_rows, n_uly, kv_columns),
            values.reshape(token_rows, n_uly, kv_columns),
        ],
        axis=2,
    ).transpose(1, 0, 2)
    kv_local = lax.all_to_all(kv_dest, "uly", split_axis=0, concat_axis=0, tiled=True)
    q_local = lax.all_to_all(q_dest, "uly", split_axis=0, concat_axis=0, tiled=True)
    block = token_rows * n_uly
    ext_off = CYCLE * block
    ext = ext_off + block
    position = lax.axis_index("blk")

    kv_local = kv_local.reshape(block, 2 * kv_columns)
    pieces = [kv_local]
    for back in range(1, CYCLE + 1):
        pieces.append(passed_along(kv_local, "blk", back))

    ends = jnp.cumsum(doc_lengths)
    starts = ends - doc_lengths
    q_pos = position * block + jnp.arange(block, dtype=jnp.int32)
    q_doc = jnp.clip(doc_index(q_pos, doc_lengths), 0, doc_lengths.shape[0] - 1)
    q_start = (starts[q_doc] - position * block + ext_off).reshape(1, block)
    bounds = tile_bounds(position, block, ext_off, ext, doc_lengths)

    q2 = q_local.reshape(block, columns)
    result = attend(bounds, q_start, q2, pieces[::-1], heads, ext_off)
    result = result.reshape(n_uly, token_rows, columns)
    returned = lax.all_to_all(result, "uly", split_axis=0, concat_axis=0, tiled=True)
    return returned.transpose(1, 0, 2).reshape(token_rows, QUERY_HEADS * HEAD_SIZE)


def solution(mesh):
    in_specs = (
        P(("dp", "blk", "uly"), None),
        P(("dp", "blk", "uly"), None),
        P(("dp", "blk", "uly"), None),
        P("dp"),
    )
    out_specs = P(("dp", "blk", "uly"), None)
    return jax.shard_map(
        per_device, mesh=mesh, in_specs=in_specs, out_specs=out_specs, check_vma=False
    )
```

```python
import functools
import math

import jax
import jax.numpy as jnp
from jax import lax
from jax.experimental import pallas as pl
from jax.experimental.pallas import tpu as pltpu
from jax.sharding import PartitionSpec as P

QUERY_HEADS = 32
KEY_VALUE_HEADS = 8
HEAD_SIZE = 128
CYCLE = 2

Q_TILE = 128
K_TILE = 512

NEG_FILL = -1e30


def passed_along(block, axis, distance):
    devices = range(lax.axis_size(axis))
    route = [(i - distance, i) for i in devices if i - distance in devices]
    return lax.ppermute(block, axis, route)


def doc_index(positions, doc_lengths):
    ends = jnp.cumsum(doc_lengths)
    return jnp.sum((positions[:, None] >= ends[None, :]).astype(jnp.int32), axis=1)


def attend_kernel(bounds_ref, q_start_ref, q_ref, b2_ref, b1_ref, own_ref, o_ref,
                  k_sc, vt_sc, peak_sc, total_sc, summed_sc, *, heads, ext_off):
    i = pl.program_id(0)
    block = own_ref.shape[0]
    per_block = block // K_TILE

    @pl.when(i == 0)
    def _():
        for p, ref in enumerate((b2_ref, b1_ref, own_ref)):
            k_sc[p * block:(p + 1) * block, :] = ref[:, :HEAD_SIZE]
            for t in range(per_block):
                v = ref[t * K_TILE:(t + 1) * K_TILE, HEAD_SIZE:].astype(jnp.float32)
                vt_sc[p * per_block + t] = v.T.astype(vt_sc.dtype)

    lo = bounds_ref[4 * i]
    mid_lo = bounds_ref[4 * i + 1]
    mid_hi = bounds_ref[4 * i + 2]
    hi = bounds_ref[4 * i + 3]
    peak_sc[...] = jnp.full(peak_sc.shape, NEG_FILL, jnp.float32)
    total_sc[...] = jnp.zeros(total_sc.shape, jnp.float32)
    summed_sc[...] = jnp.zeros(summed_sc.shape, jnp.float32)
    q_start = q_start_ref[...]
    q_col = i * Q_TILE + ext_off + lax.broadcasted_iota(jnp.int32, (1, Q_TILE), 1)
    rate = math.log2(math.e) / math.sqrt(HEAD_SIZE)

    def step(j, masked):
        start = pl.multiple_of(j * K_TILE, K_TILE)
        k = k_sc[pl.ds(start, K_TILE), :]
        vt = vt_sc[j]
        if masked:
            k_row = start + lax.broadcasted_iota(jnp.int32, (K_TILE, 1), 0)
            bias = jnp.where((k_row >= q_start) & (k_row <= q_col), 0.0, NEG_FILL)
        for h in range(heads):
            q = q_ref[:, h * HEAD_SIZE:(h + 1) * HEAD_SIZE]
            scores = lax.dot_general(
                k, q, (((1,), (1,)), ((), ())), preferred_element_type=jnp.float32
            )
            if masked:
                scores = scores + bias
            peak = peak_sc[h]
            new_peak = jnp.maximum(peak, jnp.max(scores, axis=0, keepdims=True))
            floor = jnp.maximum(new_peak, 0.1 * NEG_FILL) if masked else new_peak
            weights = jnp.exp2((scores - floor) * rate)
            factor = jnp.exp2((peak - new_peak) * rate)
            total_sc[h] = total_sc[h] * factor + jnp.sum(weights, axis=0, keepdims=True)
            summed_sc[h] = summed_sc[h] * factor + jnp.dot(
                vt, weights.astype(jnp.bfloat16), preferred_element_type=jnp.float32
            )
            peak_sc[h] = new_peak

    def masked_step(j, carry):
        step(j, True)
        return carry

    def open_step(j, carry):
        step(j, False)
        return carry

    lax.fori_loop(mid_lo, mid_hi, open_step, 0)
    lax.fori_loop(lo, mid_lo, masked_step, 0)
    lax.fori_loop(mid_hi, hi, masked_step, 0)
    for h in range(heads):
        o_ref[:, h * HEAD_SIZE:(h + 1) * HEAD_SIZE] = (
            (summed_sc[h] * (1.0 / total_sc[h])).T
        ).astype(o_ref.dtype)


def attend(bounds, q_start, q2, kv_pieces, heads, ext_off):
    rows = q2.shape[0]
    block = kv_pieces[0].shape[0]
    ext = block * len(kv_pieces)
    n_q = rows // Q_TILE
    n_k = ext // K_TILE
    kernel = functools.partial(attend_kernel, heads=heads, ext_off=ext_off)
    kv_spec = pl.BlockSpec((block, 2 * HEAD_SIZE), lambda i, b: (0, 0))
    grid_spec = pltpu.PrefetchScalarGridSpec(
        num_scalar_prefetch=1,
        grid=(n_q,),
        in_specs=[
            pl.BlockSpec((1, Q_TILE), lambda i, b: (0, i)),
            pl.BlockSpec((Q_TILE, heads * HEAD_SIZE), lambda i, b: (i, 0)),
            kv_spec,
            kv_spec,
            kv_spec,
        ],
        out_specs=pl.BlockSpec((Q_TILE, heads * HEAD_SIZE), lambda i, b: (i, 0)),
        scratch_shapes=[
            pltpu.VMEM((ext, HEAD_SIZE), jnp.bfloat16),
            pltpu.VMEM((n_k, HEAD_SIZE, K_TILE), jnp.bfloat16),
            pltpu.VMEM((heads, 1, Q_TILE), jnp.float32),
            pltpu.VMEM((heads, 1, Q_TILE), jnp.float32),
            pltpu.VMEM((heads, HEAD_SIZE, Q_TILE), jnp.float32),
        ],
    )
    return pl.pallas_call(
        kernel,
        grid_spec=grid_spec,
        out_shape=jax.ShapeDtypeStruct((rows, heads * HEAD_SIZE), jnp.bfloat16),
        compiler_params=pltpu.CompilerParams(),
    )(bounds, q_start, q2, *kv_pieces)


def tile_bounds(position, block, ext_off, ext, doc_lengths):
    ends = jnp.cumsum(doc_lengths)
    starts = ends - doc_lengths
    n_q = block // Q_TILE
    n_k = ext // K_TILE
    first_local = jnp.arange(n_q, dtype=jnp.int32) * Q_TILE
    first = position * block + first_local
    last = first + Q_TILE - 1
    first_doc = jnp.clip(doc_index(first, doc_lengths), 0, doc_lengths.shape[0] - 1)
    last_doc = doc_index(last, doc_lengths)
    start_ext = starts[first_doc] - position * block + ext_off
    lo_key = jnp.maximum(start_ext, 0)
    hi_key = first_local + Q_TILE - 1 + ext_off
    hi = jnp.clip(hi_key // K_TILE, 0, n_k - 1)
    lo = jnp.clip(lo_key // K_TILE, 0, hi)
    open_lo = (lo_key + K_TILE - 1) // K_TILE
    open_hi = (first_local + ext_off + 1) // K_TILE
    open_lo = jnp.clip(open_lo, lo, hi + 1)
    open_hi = jnp.clip(open_hi, open_lo, hi + 1)
    same = (first_doc == last_doc) & (start_ext >= 0)
    open_lo = jnp.where(same, open_lo, lo)
    open_hi = jnp.where(same, open_hi, lo)
    return jnp.stack([lo, open_lo, open_hi, hi + 1], axis=1).reshape(-1).astype(jnp.int32)


def per_device(queries, keys, values, doc_lengths):
    token_rows = queries.shape[0]
    n_uly = lax.axis_size("uly")
    heads = QUERY_HEADS // n_uly
    columns = heads * HEAD_SIZE
    kv_columns = KEY_VALUE_HEADS * HEAD_SIZE // n_uly
    q_dest = queries.reshape(token_rows, n_uly, columns).transpose(1, 0, 2)
    kv_dest = jnp.concatenate(
        [
            keys.reshape(token_rows, n_uly, kv_columns),
            values.reshape(token_rows, n_uly, kv_columns),
        ],
        axis=2,
    ).transpose(1, 0, 2)
    kv_local = lax.all_to_all(kv_dest, "uly", split_axis=0, concat_axis=0, tiled=True)
    q_local = lax.all_to_all(q_dest, "uly", split_axis=0, concat_axis=0, tiled=True)
    block = token_rows * n_uly
    ext_off = CYCLE * block
    ext = ext_off + block
    position = lax.axis_index("blk")

    kv_local = kv_local.reshape(block, 2 * kv_columns)
    pieces = [kv_local]
    for back in range(1, CYCLE + 1):
        pieces.append(passed_along(kv_local, "blk", back))

    ends = jnp.cumsum(doc_lengths)
    starts = ends - doc_lengths
    q_pos = position * block + jnp.arange(block, dtype=jnp.int32)
    q_doc = jnp.clip(doc_index(q_pos, doc_lengths), 0, doc_lengths.shape[0] - 1)
    q_start = (starts[q_doc] - position * block + ext_off).reshape(1, block)
    bounds = tile_bounds(position, block, ext_off, ext, doc_lengths)

    q2 = q_local.reshape(block, columns)
    result = attend(bounds, q_start, q2, pieces[::-1], heads, ext_off)
    result = result.reshape(n_uly, token_rows, columns)
    returned = lax.all_to_all(result, "uly", split_axis=0, concat_axis=0, tiled=True)
    return returned.transpose(1, 0, 2).reshape(token_rows, QUERY_HEADS * HEAD_SIZE)


def solution(mesh):
    in_specs = (
        P(("dp", "blk", "uly"), None),
        P(("dp", "blk", "uly"), None),
        P(("dp", "blk", "uly"), None),
        P("dp"),
    )
    out_specs = P(("dp", "blk", "uly"), None)
    return jax.shard_map(
        per_device, mesh=mesh, in_specs=in_specs, out_specs=out_specs, check_vma=False
    )
```

```python
import functools
import math

import jax
import jax.numpy as jnp
from jax import lax
from jax.experimental import pallas as pl
from jax.experimental.pallas import tpu as pltpu
from jax.sharding import PartitionSpec as P

QUERY_HEADS = 32
KEY_VALUE_HEADS = 8
HEAD_SIZE = 128
CYCLE = 2

Q_TILE = 128
K_TILE = 512

NEG_FILL = -1e30


def passed_along(block, axis, distance):
    devices = range(lax.axis_size(axis))
    route = [(i - distance, i) for i in devices if i - distance in devices]
    return lax.ppermute(block, axis, route)


def doc_index(positions, doc_lengths):
    ends = jnp.cumsum(doc_lengths)
    return jnp.sum((positions[:, None] >= ends[None, :]).astype(jnp.int32), axis=1)


def attend_kernel(bounds_ref, q_start_ref, q_ref, b2_ref, b1_ref, own_ref, o_ref,
                  k_sc, vt_sc, peak_sc, total_sc, summed_sc, *, heads, ext_off):
    i = pl.program_id(0)
    block = own_ref.shape[0]
    per_block = block // K_TILE

    @pl.when(i == 0)
    def _():
        for p, ref in enumerate((b2_ref, b1_ref, own_ref)):
            k_sc[p * block:(p + 1) * block, :] = ref[:, :HEAD_SIZE]
            for t in range(per_block):
                v = ref[t * K_TILE:(t + 1) * K_TILE, HEAD_SIZE:].astype(jnp.float32)
                vt_sc[p * per_block + t] = v.T.astype(vt_sc.dtype)

    lo = bounds_ref[4 * i]
    mid_lo = bounds_ref[4 * i + 1]
    mid_hi = bounds_ref[4 * i + 2]
    hi = bounds_ref[4 * i + 3]
    peak_sc[...] = jnp.full(peak_sc.shape, NEG_FILL, jnp.float32)
    total_sc[...] = jnp.zeros(total_sc.shape, jnp.float32)
    summed_sc[...] = jnp.zeros(summed_sc.shape, jnp.float32)
    q_start = q_start_ref[...]
    q_col = i * Q_TILE + ext_off + lax.broadcasted_iota(jnp.int32, (1, Q_TILE), 1)
    rate = math.log2(math.e) / math.sqrt(HEAD_SIZE)

    def step(j, masked):
        start = pl.multiple_of(j * K_TILE, K_TILE)
        k = k_sc[pl.ds(start, K_TILE), :]
        vt = vt_sc[j]
        if masked:
            k_row = start + lax.broadcasted_iota(jnp.int32, (K_TILE, 1), 0)
            bias = jnp.where((k_row >= q_start) & (k_row <= q_col), 0.0, NEG_FILL)
        for h in range(heads):
            q = q_ref[:, h * HEAD_SIZE:(h + 1) * HEAD_SIZE]
            scores = lax.dot_general(
                k, q, (((1,), (1,)), ((), ())), preferred_element_type=jnp.float32
            )
            if masked:
                scores = scores + bias
            peak = peak_sc[h]
            new_peak = jnp.maximum(peak, jnp.max(scores, axis=0, keepdims=True))
            floor = jnp.maximum(new_peak, 0.1 * NEG_FILL) if masked else new_peak
            weights = jnp.exp2((scores - floor) * rate)
            factor = jnp.exp2((peak - new_peak) * rate)
            total_sc[h] = total_sc[h] * factor + jnp.sum(weights, axis=0, keepdims=True)
            summed_sc[h] = summed_sc[h] * factor + jnp.dot(
                vt, weights.astype(jnp.bfloat16), preferred_element_type=jnp.float32
            )
            peak_sc[h] = new_peak

    def masked_step(j, carry):
        step(j, True)
        return carry

    def open_step(j, carry):
        step(j, False)
        return carry

    lax.fori_loop(mid_lo, mid_hi, open_step, 0)
    lax.fori_loop(lo, mid_lo, masked_step, 0)
    lax.fori_loop(mid_hi, hi, masked_step, 0)
    for h in range(heads):
        o_ref[:, h * HEAD_SIZE:(h + 1) * HEAD_SIZE] = (
            (summed_sc[h] * (1.0 / total_sc[h])).T
        ).astype(o_ref.dtype)


def attend(bounds, q_start, q2, kv_pieces, heads, ext_off):
    rows = q2.shape[0]
    block = kv_pieces[0].shape[0]
    ext = block * len(kv_pieces)
    n_q = rows // Q_TILE
    n_k = ext // K_TILE
    kernel = functools.partial(attend_kernel, heads=heads, ext_off=ext_off)
    kv_spec = pl.BlockSpec((block, 2 * HEAD_SIZE), lambda i, b: (0, 0))
    grid_spec = pltpu.PrefetchScalarGridSpec(
        num_scalar_prefetch=1,
        grid=(n_q,),
        in_specs=[
            pl.BlockSpec((1, Q_TILE), lambda i, b: (0, i)),
            pl.BlockSpec((Q_TILE, heads * HEAD_SIZE), lambda i, b: (i, 0)),
            kv_spec,
            kv_spec,
            kv_spec,
        ],
        out_specs=pl.BlockSpec((Q_TILE, heads * HEAD_SIZE), lambda i, b: (i, 0)),
        scratch_shapes=[
            pltpu.VMEM((ext, HEAD_SIZE), jnp.bfloat16),
            pltpu.VMEM((n_k, HEAD_SIZE, K_TILE), jnp.bfloat16),
            pltpu.VMEM((heads, 1, Q_TILE), jnp.float32),
            pltpu.VMEM((heads, 1, Q_TILE), jnp.float32),
            pltpu.VMEM((heads, HEAD_SIZE, Q_TILE), jnp.float32),
        ],
    )
    return pl.pallas_call(
        kernel,
        grid_spec=grid_spec,
        out_shape=jax.ShapeDtypeStruct((rows, heads * HEAD_SIZE), jnp.bfloat16),
        compiler_params=pltpu.CompilerParams(),
    )(bounds, q_start, q2, *kv_pieces)


def doc_start(positions, doc_lengths):
    ends = jnp.cumsum(doc_lengths)
    return jnp.max(jnp.where(ends[None, :] <= positions[:, None], ends[None, :], 0), axis=1)


def tile_bounds(position, block, ext_off, ext, doc_lengths):
    n_q = block // Q_TILE
    n_k = ext // K_TILE
    first_local = jnp.arange(n_q, dtype=jnp.int32) * Q_TILE
    first = position * block + first_local
    last = first + Q_TILE - 1
    first_start = doc_start(first, doc_lengths)
    last_start = doc_start(last, doc_lengths)
    start_ext = first_start - position * block + ext_off
    lo_key = jnp.maximum(start_ext, 0)
    hi_key = first_local + Q_TILE - 1 + ext_off
    hi = jnp.clip(hi_key // K_TILE, 0, n_k - 1)
    lo = jnp.clip(lo_key // K_TILE, 0, hi)
    open_lo = (lo_key + K_TILE - 1) // K_TILE
    open_hi = (first_local + ext_off + 1) // K_TILE
    open_lo = jnp.clip(open_lo, lo, hi + 1)
    open_hi = jnp.clip(open_hi, open_lo, hi + 1)
    same = (first_start == last_start) & (start_ext >= 0)
    open_lo = jnp.where(same, open_lo, lo)
    open_hi = jnp.where(same, open_hi, lo)
    return jnp.stack([lo, open_lo, open_hi, hi + 1], axis=1).reshape(-1).astype(jnp.int32)


def per_device(queries, keys, values, doc_lengths):
    token_rows = queries.shape[0]
    n_uly = lax.axis_size("uly")
    heads = QUERY_HEADS // n_uly
    columns = heads * HEAD_SIZE
    kv_columns = KEY_VALUE_HEADS * HEAD_SIZE // n_uly
    q_dest = queries.reshape(token_rows, n_uly, columns).transpose(1, 0, 2)
    kv_dest = jnp.concatenate(
        [
            keys.reshape(token_rows, n_uly, kv_columns),
            values.reshape(token_rows, n_uly, kv_columns),
        ],
        axis=2,
    ).transpose(1, 0, 2)
    kv_local = lax.all_to_all(kv_dest, "uly", split_axis=0, concat_axis=0, tiled=True)
    q_local = lax.all_to_all(q_dest, "uly", split_axis=0, concat_axis=0, tiled=True)
    block = token_rows * n_uly
    ext_off = CYCLE * block
    ext = ext_off + block
    position = lax.axis_index("blk")

    kv_local = kv_local.reshape(block, 2 * kv_columns)
    pieces = [kv_local]
    for back in range(1, CYCLE + 1):
        pieces.append(passed_along(kv_local, "blk", back))

    q_pos = position * block + jnp.arange(block, dtype=jnp.int32)
    q_start = (doc_start(q_pos, doc_lengths) - position * block + ext_off).reshape(1, block)
    bounds = tile_bounds(position, block, ext_off, ext, doc_lengths)

    q2 = q_local.reshape(block, columns)
    result = attend(bounds, q_start, q2, pieces[::-1], heads, ext_off)
    result = result.reshape(n_uly, token_rows, columns)
    returned = lax.all_to_all(result, "uly", split_axis=0, concat_axis=0, tiled=True)
    return returned.transpose(1, 0, 2).reshape(token_rows, QUERY_HEADS * HEAD_SIZE)


def solution(mesh):
    in_specs = (
        P(("dp", "blk", "uly"), None),
        P(("dp", "blk", "uly"), None),
        P(("dp", "blk", "uly"), None),
        P("dp"),
    )
    out_specs = P(("dp", "blk", "uly"), None)
    return jax.shard_map(
        per_device, mesh=mesh, in_specs=in_specs, out_specs=out_specs, check_vma=False
    )
```
